512 devices in a mesh: sub: 8 (over x, core), seq: 8 (over y), exp: 8 (over z).
Axes of the slice: x: 4, y: 8, z: 8, core: 2. Of those that a mesh axis runs over, the one named last changes fastest.
Arguments:
- node_features: bfloat16 [64, 1536, 1024], P(('sub', 'exp'), 'seq'), parts along dimension 0, may hold values from -24 to 24
- block_mask: int32 [64, 12, 12], P(('sub', 'exp')), parts along dimension 0, may hold values from 0 to 1, as said below
- w_qkv: bfloat16 [1024, 3072], P('exp', 'seq'), may hold values from -4 to 4
- w_out: bfloat16 [1024, 1024], P('seq', 'exp'), may hold values from -0.1875 to 0.1875
- norm_gain: float32 [1024], replicated, may hold values from 0.5 to 1.5
- routes: int32 [64, 1536, 2], P(('sub', 'exp'), 'seq'), parts along dimension 0, may hold values from 0 to 63, all different within a row; in each aligned block of 192 rows (0 to 191, 192 to 383, ..., all dimensions but the last counted through in order) at most 12 rows name the same one
- gates: float32 [64, 1536, 2], P(('sub', 'exp'), 'seq'), parts along dimension 0, may hold values from 0.1 to 1
- w_gate_up: bfloat16 [64, 1024, 1024], P(('seq', 'exp')), may hold values from -0.1875 to 0.1875
- w_down: bfloat16 [64, 512, 1024], P(('seq', 'exp')), may hold values from -0.25 to 0.25
Outputs:
- layer_out: bfloat16 [64, 1536, 1024], P(('sub', 'exp'), 'seq'), parts along dimension 0
The draws below stay inside these ranges and needn't reach their ends.
There are 8 independent parts, one for each index of `sub`. The reference program is written for one: setup_inputs(seed, part) draws one part's arguments, and reference() takes and returns one part's arrays. A program takes and returns all parts, laid end to end along the dimension named above; an argument that names none is the same for every part. Nothing has to cross between parts.
Inputs may be any that keep to these rules, and one draw needn't show every extreme that they name: In each aligned block of 192 rows (one device's nodes, subgraphs then nodes in order) no expert is named by more than 12 of the rows' routes, a bound that some block reaches; the 2 experts of a node differ. `block_mask`: the diagonal blocks are 1.
All inputs are finite; a program needn't handle non-finite values.
Results may differ from the reference program's by a relative error of at most 0.0065.
The reference program's roundings to bfloat16 on the way count: a program that leaves them out, or rounds other values in their place, can miss the bound.
Values may be sent and summed in bfloat16 or wider, within the bound.
No kernel may reach another device: no remote copies, remote signals or barrier semaphores. Data moves between devices by JAX's collectives and lax.ppermute only.
A program may use at most 64 MiB of HBM per device.

```python
import math
import jax
import jax.numpy as jnp
import numpy as np
from jax import lax

D = 1024
HEADS = 16
HEAD_DIM = 64
FF = 512
TOP = 2
BLOCK = 128
NODE_DEV = 192
SUBG = 8
NODES = 1536
EXPERTS = 64
CAP = 12


def draw_node_features(key, part):
    shape = (SUBG, NODES, D)
    base = jnp.clip(jax.random.normal(key, shape, jnp.float32), -5.0, 5.0)
    return base.astype(jnp.bfloat16)


def draw_w_qkv(key, part):
    base = jnp.clip(jax.random.normal(key, (D, HEADS, 3, HEAD_DIM), jnp.float32), -6.0, 6.0) * D ** (-0.5)
    return base.reshape(D, 3 * D).astype(jnp.bfloat16)


def draw_block_mask(key, part):
    count = NODES // BLOCK
    density_key = jax.random.fold_in(key, 21)
    rolls_key = jax.random.fold_in(key, 22)
    density = jax.random.randint(density_key, (SUBG, 1, 1), 15, 90)
    rolls = jax.random.randint(rolls_key, (SUBG, count, count), 0, 100)
    diagonal = jnp.eye(count, dtype=jnp.int32)[None]
    return jnp.maximum((rolls < density).astype(jnp.int32), diagonal)


def block_levels(key, dims, cuts, smallest, largest):
    def one(dim, parts):
        steps = jax.random.uniform(jax.random.fold_in(jax.random.fold_in(key, 6), dim), (parts,), jnp.float32, smallest / len(cuts), largest / len(cuts))
        return jnp.repeat(jnp.exp(steps), dims[dim] // parts).reshape((-1,) + (1,) * (len(dims) - dim - 1))

    loudness = one(*cuts[0])
    for cut in cuts[1:]:
        loudness = loudness * one(*cut)
    return loudness


def deal_out(key, own, number, rows, count, top, reach, slope):
    ranking = jax.random.permutation(key, count)
    heavy_load, usual = portions_of(count, rows * top, reach, slope, True), portions_of(count, rows * top, reach, slope, False)
    places = jnp.arange(count)

    def named(tallies, offset_by):
        used = int((tallies > 0).sum())
        fixed = max(1, used // 4)
        passed = fixed + (places - fixed + offset_by * (used - fixed)) % max(1, count - fixed)
        return jnp.zeros((count,), jnp.int32).at[ranking[jnp.where(places < fixed, places, passed)]].set(jnp.asarray(tallies, jnp.int32))

    tallies = jnp.where(number % 4 == 0, named(heavy_load, number // 4), named(usual, number - number // 4 - 1))
    mixed = jax.random.permutation(jax.random.fold_in(own, 3), count)
    giver, sink = mixed[0:count // 2 * 2:2], mixed[1:count // 2 * 2:2]
    margin = jnp.minimum(tallies[giver] - 1, reach - tallies[sink]) // 2
    margin = jnp.where((giver == ranking[0]) | (sink == ranking[0]) | (tallies[sink] == 0), 0, jnp.maximum(margin, 0))
    passed = jax.random.randint(jax.random.fold_in(own, 4), (count // 2,), 0, 1 << 20) % (margin + 1)
    tallies = tallies.at[giver].add(-passed).at[sink].add(passed)
    items = jnp.searchsorted(jnp.cumsum(tallies), jnp.arange(rows * top), side="right").astype(jnp.int32)
    listing = items.reshape(top, rows).T
    listing = listing[jax.random.permutation(jax.random.fold_in(own, 1), rows)]
    offset_by = jax.random.randint(jax.random.fold_in(own, 2), (rows, 1), 0, top)
    return jnp.take_along_axis(listing, (jnp.arange(top)[None, :] + offset_by) % top, axis=1)


def portions_of(count, total, bound, slope, full):
    weights = [(1 << 20) // math.isqrt(grade ** slope) + 1 for grade in range(1, count + 1)]
    largest = bound if full else min(bound, max(-(-total // count), total * weights[0] // sum(weights)))
    least = 1 if total - largest >= count - 1 else 0
    holding, rest = [largest] + [least] * (count - 1), total - largest - least * (count - 1)
    while rest > 0:
        candidates = [i for i in range(1, count) if holding[i] < largest] or [i for i in range(1, count) if holding[i] < bound]
        whole, budget = sum([weights[i] for i in candidates]), rest
        for i in candidates:
            addition = min(bound - holding[i], max(1, budget * weights[i] // whole), rest)
            holding[i] = holding[i] + addition
            rest = rest - addition
    return np.array(holding)


def gaussian(rng, extent, spread, most, cuts=(), kind=jnp.bfloat16):
    array = spread * jax.random.normal(rng, extent, jnp.float32)
    if cuts:
        array = array * block_levels(rng, extent, cuts, -0.22, 0.18)
    return jnp.clip(array, -most, most).astype(kind)


def setup_inputs(seed: int = 0, part: int = 0) -> dict:
    streams_of = jax.random.split(jax.random.key(seed), 10)
    own_keys = jax.random.split(jax.random.fold_in(streams_of[9], part), 10)
    node_features = draw_node_features(jax.random.fold_in(jax.random.fold_in(streams_of[9], part), 71), part)
    block_mask = draw_block_mask(jax.random.fold_in(jax.random.fold_in(streams_of[9], part), 71), part)
    w_qkv = draw_w_qkv(jax.random.fold_in(streams_of[9], 71), part)
    w_out = gaussian(streams_of[3], (D, D), D ** -0.5, 0.1875, ((0, 8), (1, 8)))
    norm_gain = jnp.clip(1.0 + 0.1 * jax.random.normal(streams_of[4], (D,), jnp.float32), 0.5, 1.5)
    routes_keys = jax.random.split(jax.random.fold_in(own_keys[5], 1), SUBG * NODES // NODE_DEV)
    routes_turns = jax.random.permutation(jax.random.fold_in(own_keys[5], 3), SUBG * NODES // NODE_DEV)
    routes = jax.vmap(lambda own, number: deal_out(jax.random.fold_in(own_keys[5], 2), own, number, NODE_DEV, EXPERTS, TOP, CAP, 2))(routes_keys, routes_turns).reshape((SUBG, NODES, TOP))
    gates = jnp.clip(0.1 + 0.9 * jax.random.uniform(own_keys[6], (SUBG, NODES, TOP), jnp.float32) ** block_levels(own_keys[6], (SUBG, NODES, TOP), ((0, 8), (1, 8)), -0.2, 0.2), 0.1, 1.0)
    w_gate_up = gaussian(streams_of[7], (EXPERTS, D, 2 * FF), D ** -0.5, 0.1875, ((0, 64),))
    w_down = gaussian(streams_of[8], (EXPERTS, FF, D), FF ** -0.5, 0.25, ((0, 64),))
    return {"node_features": node_features, "block_mask": block_mask, "w_qkv": w_qkv, "w_out": w_out, "norm_gain": norm_gain, "routes": routes, "gates": gates, "w_gate_up": w_gate_up, "w_down": w_down}


def reference(node_features, block_mask, w_qkv, w_out, norm_gain, routes, gates, w_gate_up, w_down):
    scale = 1.0 / math.sqrt(HEAD_DIM)

    def one_graph(item):
        feats, mask = item
        qkv = jnp.dot(feats, w_qkv, preferred_element_type=jnp.float32).astype(jnp.bfloat16)
        split = qkv.reshape(NODES, HEADS, 3, HEAD_DIM).astype(jnp.float32)
        query = split[:, :, 0]
        keys = split[:, :, 1]
        values = split[:, :, 2]
        allowed = jnp.repeat(jnp.repeat(mask, BLOCK, axis=0), BLOCK, axis=1) > 0
        scores = jnp.einsum('qhd,khd->hqk', query, keys) * scale
        scores = jnp.where(allowed[None], scores, -1e+30)
        top = lax.optimization_barrier(jnp.max(scores, axis=-1, keepdims=True))
        weights = jnp.exp(scores - top)
        probs = (weights / lax.optimization_barrier(jnp.sum(weights, axis=-1, keepdims=True))).astype(jnp.bfloat16)
        attended = jnp.einsum('hqk,khd->qhd', probs.astype(jnp.float32), values).astype(jnp.bfloat16)
        attended = attended.reshape(NODES, D)
        return feats.astype(jnp.float32) + jnp.dot(attended, w_out, preferred_element_type=jnp.float32)
    mixed = lax.map(one_graph, (node_features, block_mask))
    mean_square = lax.optimization_barrier(jnp.mean(mixed * mixed, axis=-1, keepdims=True))
    normed = (mixed * lax.rsqrt(mean_square + 1e-06) * norm_gain).astype(jnp.bfloat16)
    sources = SUBG * NODES // NODE_DEV
    pairs = NODE_DEV * TOP
    flat_routes = routes.reshape(sources, pairs).astype(jnp.int32)
    onehot = (flat_routes[:, :, None] == jnp.arange(EXPERTS, dtype=jnp.int32)).astype(jnp.int32)
    earlier = jnp.cumsum(onehot, axis=1, dtype=jnp.int32) - onehot
    slots = lax.optimization_barrier(jnp.sum(earlier * onehot, axis=-1, dtype=jnp.int32))
    position = (jnp.arange(sources, dtype=jnp.int32)[:, None] * CAP + slots).astype(jnp.int32)
    rows = jnp.repeat(normed.reshape(sources, NODE_DEV, D), TOP, axis=1)
    buffer = jnp.zeros((EXPERTS, sources * CAP, D), jnp.bfloat16).at[flat_routes, position].set(rows)

    def one_expert(item):
        block, gate_up, down = item
        both = jnp.dot(block, gate_up, preferred_element_type=jnp.float32)
        hidden = (jax.nn.silu(both[:, :FF]) * both[:, FF:]).astype(jnp.bfloat16)
        return jnp.dot(hidden, down, preferred_element_type=jnp.float32).astype(jnp.bfloat16)
    results = lax.map(one_expert, (buffer, w_gate_up, w_down))
    picked = results[flat_routes, position].astype(jnp.float32).reshape(SUBG, NODES, TOP, D)
    moe = lax.optimization_barrier(jnp.sum(picked * gates[..., None], axis=2))
    return (mixed + moe).astype(jnp.bfloat16)
```

```python
import math

import jax
import jax.numpy as jnp
from jax import lax
from jax.sharding import PartitionSpec as P

HEAD_DIM = 64
TOP = 2
BLOCK = 128


def per_device(
    node_features, block_mask, w_qkv, w_out, norm_gain, routes, gates, w_gate_up, w_down
):
    feats = node_features[0]
    node_dev, width = feats.shape
    seq_count = lax.axis_size("seq")
    exp_count = lax.axis_size("exp")
    experts = seq_count * exp_count * w_gate_up.shape[0]
    head_cols = w_qkv.shape[1]
    cols_slice = lax.all_gather(w_qkv, "exp", axis=0, tiled=True)
    out_rows = lax.all_gather(w_out[None], "exp", axis=0, tiled=True)
    out_all = lax.all_gather(out_rows[None], "seq", axis=0, tiled=True)
    me = lax.axis_index("seq")
    right = [(i, (i + 1) % seq_count) for i in range(seq_count)]
    left = [(i, (i - 1) % seq_count) for i in range(seq_count)]
    relative = [None] * seq_count
    relative[0] = feats
    moving_r, moving_l = feats, feats
    for step in range(1, seq_count // 2 + 1):
        moving_r = lax.ppermute(moving_r, "seq", right)
        relative[(seq_count - step) % seq_count] = moving_r
        if step < seq_count - step:
            moving_l = lax.ppermute(moving_l, "seq", left)
            relative[step] = moving_l
    stacked = jnp.stack(relative)
    order = (jnp.arange(seq_count, dtype=jnp.int32) - me) % seq_count
    gathered = jnp.take(stacked, order, axis=0).reshape(seq_count * node_dev, width)
    projected = jnp.dot(gathered, cols_slice, preferred_element_type=jnp.float32).astype(
        jnp.bfloat16
    )
    nodes = projected.shape[0]
    heads_here = head_cols // (3 * HEAD_DIM)
    split = projected.reshape(nodes, heads_here, 3, HEAD_DIM)
    query = split[:, :, 0]
    keys = split[:, :, 1]
    values = split[:, :, 2]
    col_mask = jnp.repeat(block_mask[0], BLOCK, axis=1) > 0
    span = math.gcd(nodes, 512)
    scale = 1.0 / math.sqrt(HEAD_DIM)

    def attend(index):
        start = index * span
        rows_query = lax.dynamic_slice_in_dim(query, start, span, 0)
        rows_mask = lax.dynamic_slice_in_dim(col_mask, start // BLOCK, span // BLOCK, 0)
        allowed = jnp.repeat(rows_mask, BLOCK, axis=0)
        scores = (
            jnp.einsum("qhd,khd->hqk", rows_query, keys, preferred_element_type=jnp.float32) * scale
        )
        scores = jnp.where(allowed[None], scores, -1e30)
        top = jnp.max(scores, axis=-1, keepdims=True)
        weights = jnp.exp(scores - top)
        probs = (weights / jnp.sum(weights, axis=-1, keepdims=True)).astype(jnp.bfloat16)
        return jnp.einsum("hqk,khd->qhd", probs, values, preferred_element_type=jnp.float32).astype(
            jnp.bfloat16
        )

    blocks = lax.map(attend, jnp.arange(nodes // span, dtype=jnp.int32))
    attended = blocks.reshape(nodes, heads_here * HEAD_DIM)
    node_attended = lax.all_to_all(attended, "seq", split_axis=0, concat_axis=1, tiled=True)
    out_tiles = out_all
    attn_out = jnp.einsum(
        "nsk,sekc->nec",
        node_attended.reshape(node_dev, seq_count, w_out.shape[0]),
        out_tiles,
        preferred_element_type=jnp.float32,
    )
    mixed = feats.astype(jnp.float32) + attn_out.reshape(node_dev, width)
    mean_square = jnp.mean(mixed * mixed, axis=-1, keepdims=True)
    normed = (mixed * lax.rsqrt(mean_square + 1e-06) * norm_gain).astype(jnp.bfloat16)
    capacity = 2 * TOP * node_dev // experts
    pair_routes = routes[0].reshape(node_dev * TOP)
    onehot = (pair_routes[:, None] == jnp.arange(experts, dtype=jnp.int32)).astype(jnp.int32)
    earlier = jnp.cumsum(onehot, axis=0, dtype=jnp.int32) - onehot
    slots = jnp.sum(earlier * onehot, axis=1, dtype=jnp.int32)
    position = pair_routes * capacity + slots
    outgoing = (
        jnp.zeros((experts * capacity, width), jnp.bfloat16)
        .at[position]
        .set(jnp.repeat(normed, TOP, axis=0))
    )
    outgoing = outgoing.reshape(experts, capacity, width)
    hidden_units = w_down.shape[1]
    received = lax.all_to_all(outgoing, ("seq", "exp"), split_axis=0, concat_axis=0, tiled=True)
    sources, items, columns = received.shape
    flat_rows = received.reshape(sources * items, columns)
    both = jnp.dot(flat_rows, w_gate_up[0], preferred_element_type=jnp.float32)
    hidden = (jax.nn.silu(both[:, :hidden_units]) * both[:, hidden_units:]).astype(jnp.bfloat16)
    result = jnp.dot(hidden, w_down[0], preferred_element_type=jnp.float32).astype(jnp.bfloat16)
    processed = result.reshape(sources, items, columns)
    returned = lax.all_to_all(
        processed, ("seq", "exp"), split_axis=0, concat_axis=0, tiled=True
    ).reshape(experts * capacity, width)
    picked = returned[position].astype(jnp.float32).reshape(node_dev, TOP, width)
    expert_sum = jnp.sum(picked * gates[0][:, :, None], axis=1)
    return (mixed + expert_sum).astype(jnp.bfloat16)[None]


def solution(mesh):
    in_specs = (
        P(("sub", "exp"), "seq", None),
        P(("sub", "exp"), None, None),
        P("exp", "seq"),
        P("seq", "exp"),
        P(),
        P(("sub", "exp"), "seq", None),
        P(("sub", "exp"), "seq", None),
        P(("seq", "exp"), None, None),
        P(("seq", "exp"), None, None),
    )
    out_specs = P(("sub", "exp"), "seq", None)
    return jax.shard_map(
        per_device, mesh=mesh, in_specs=in_specs, out_specs=out_specs, check_vma=False
    )
```

```python
import math

import jax
import jax.numpy as jnp
from jax import lax
from jax.sharding import PartitionSpec as P

HEAD_DIM = 64
TOP = 2
BLOCK = 128


def ring_gather(piece, axis, count):
    right = [(i, (i + 1) % count) for i in range(count)]
    left = [(i, (i - 1) % count) for i in range(count)]
    relative = [None] * count
    relative[0] = piece
    moving_r, moving_l = piece, piece
    for step in range(1, count // 2 + 1):
        moving_r = lax.ppermute(moving_r, axis, right)
        relative[(count - step) % count] = moving_r
        if step < count - step:
            moving_l = lax.ppermute(moving_l, axis, left)
            relative[step] = moving_l
    return relative


def in_order(relative, axis, count):
    me = lax.axis_index(axis)
    order = (jnp.arange(count, dtype=jnp.int32) - me) % count
    return jnp.take(jnp.stack(relative), order, axis=0)


def per_device(
    node_features, block_mask, w_qkv, w_out, norm_gain, routes, gates, w_gate_up, w_down
):
    feats = node_features[0]
    node_dev, width = feats.shape
    seq_count = lax.axis_size("seq")
    exp_count = lax.axis_size("exp")
    experts = seq_count * exp_count * w_gate_up.shape[0]
    head_cols = w_qkv.shape[1]
    out_all = lax.all_gather(w_out[None], ("seq", "exp"), axis=0, tiled=True)
    cols_slice = in_order(ring_gather(w_qkv, "exp", exp_count), "exp", exp_count)
    cols_slice = cols_slice.reshape(exp_count * w_qkv.shape[0], head_cols)
    chunks = ring_gather(feats, "seq", seq_count)
    projected_rel = [
        jnp.dot(chunk, cols_slice, preferred_element_type=jnp.float32).astype(jnp.bfloat16)
        for chunk in chunks
    ]
    projected = in_order(projected_rel, "seq", seq_count).reshape(seq_count * node_dev, head_cols)
    nodes = projected.shape[0]
    heads_here = head_cols // (3 * HEAD_DIM)
    split = projected.reshape(nodes, heads_here, 3, HEAD_DIM)
    query = split[:, :, 0]
    keys = split[:, :, 1]
    values = split[:, :, 2]
    col_mask = jnp.repeat(block_mask[0], BLOCK, axis=1) > 0
    span = math.gcd(nodes, 512)
    scale = 1.0 / math.sqrt(HEAD_DIM)

    def attend(index):
        start = index * span
        rows_query = lax.dynamic_slice_in_dim(query, start, span, 0)
        rows_mask = lax.dynamic_slice_in_dim(col_mask, start // BLOCK, span // BLOCK, 0)
        allowed = jnp.repeat(rows_mask, BLOCK, axis=0)
        scores = (
            jnp.einsum("qhd,khd->hqk", rows_query, keys, preferred_element_type=jnp.float32) * scale
        )
        scores = jnp.where(allowed[None], scores, -1e30)
        top = jnp.max(scores, axis=-1, keepdims=True)
        weights = jnp.exp(scores - top)
        probs = (weights / jnp.sum(weights, axis=-1, keepdims=True)).astype(jnp.bfloat16)
        return jnp.einsum("hqk,khd->qhd", probs, values, preferred_element_type=jnp.float32).astype(
            jnp.bfloat16
        )

    blocks = lax.map(attend, jnp.arange(nodes // span, dtype=jnp.int32))
    attended = blocks.reshape(nodes, heads_here * HEAD_DIM)
    node_attended = lax.all_to_all(attended, "seq", split_axis=0, concat_axis=1, tiled=True)
    out_tiles = out_all.reshape(seq_count, exp_count, w_out.shape[0], w_out.shape[1])
    attn_out = jnp.einsum(
        "nsk,sekc->nec",
        node_attended.reshape(node_dev, seq_count, w_out.shape[0]),
        out_tiles,
        preferred_element_type=jnp.float32,
    )
    mixed = feats.astype(jnp.float32) + attn_out.reshape(node_dev, width)
    mean_square = jnp.mean(mixed * mixed, axis=-1, keepdims=True)
    normed = (mixed * lax.rsqrt(mean_square + 1e-06) * norm_gain).astype(jnp.bfloat16)
    capacity = 2 * TOP * node_dev // experts
    pair_routes = routes[0].reshape(node_dev * TOP)
    onehot = (pair_routes[:, None] == jnp.arange(experts, dtype=jnp.int32)).astype(jnp.int32)
    earlier = jnp.cumsum(onehot, axis=0, dtype=jnp.int32) - onehot
    slots = jnp.sum(earlier * onehot, axis=1, dtype=jnp.int32)
    position = (pair_routes * capacity + slots).reshape(node_dev, TOP)
    places = jnp.arange(experts * capacity, dtype=jnp.int32).reshape(experts, capacity)
    select = (places[:, :, None, None] == position[None, None]).astype(jnp.bfloat16)
    outgoing = jnp.einsum(
        "ecn,nd->ecd", jnp.sum(select, axis=3), normed, preferred_element_type=jnp.float32
    ).astype(jnp.bfloat16)
    hidden_units = w_down.shape[1]
    received = lax.all_to_all(outgoing, ("seq", "exp"), split_axis=0, concat_axis=0, tiled=True)
    both = jnp.einsum("eck,kf->ecf", received, w_gate_up[0], preferred_element_type=jnp.float32)
    hidden = (jax.nn.silu(both[..., :hidden_units]) * both[..., hidden_units:]).astype(jnp.bfloat16)
    processed = jnp.einsum(
        "ecf,fd->ecd", hidden, w_down[0], preferred_element_type=jnp.float32
    ).astype(jnp.bfloat16)
    returned = lax.all_to_all(processed, ("seq", "exp"), split_axis=0, concat_axis=0, tiled=True)
    picked = jnp.einsum("ecnk,ecd->knd", select, returned, preferred_element_type=jnp.float32)
    expert_sum = picked[0] * gates[0][:, 0, None] + picked[1] * gates[0][:, 1, None]
    return (mixed + expert_sum).astype(jnp.bfloat16)[None]


def solution(mesh):
    in_specs = (
        P(("sub", "exp"), "seq", None),
        P(("sub", "exp"), None, None),
        P("exp", "seq"),
        P("seq", "exp"),
        P(),
        P(("sub", "exp"), "seq", None),
        P(("sub", "exp"), "seq", None),
        P(("seq", "exp"), None, None),
        P(("seq", "exp"), None, None),
    )
    out_specs = P(("sub", "exp"), "seq", None)
    return jax.shard_map(
        per_device, mesh=mesh, in_specs=in_specs, out_specs=out_specs, check_vma=False
    )
```

```python
import math

import jax
import jax.numpy as jnp
from jax import lax
from jax.sharding import PartitionSpec as P

HEAD_DIM = 64
TOP = 2
BLOCK = 128


def ring_gather(pieces, axes, counts):
    relatives = [[piece] + [None] * (count - 1) for piece, count in zip(pieces, counts)]
    moving = [[piece, piece] for piece in pieces]
    for step in range(1, max(counts) // 2 + 1):
        for which, (axis, count) in enumerate(zip(axes, counts)):
            if step > count // 2:
                continue
            right = [(i, (i + 1) % count) for i in range(count)]
            left = [(i, (i - 1) % count) for i in range(count)]
            moving[which][0] = lax.ppermute(moving[which][0], axis, right)
            relatives[which][(count - step) % count] = moving[which][0]
            if step < count - step:
                moving[which][1] = lax.ppermute(moving[which][1], axis, left)
                relatives[which][step] = moving[which][1]
        moving = lax.optimization_barrier(moving)
        for which, count in enumerate(counts):
            if step <= count // 2:
                relatives[which][(count - step) % count] = moving[which][0]
                if step < count - step:
                    relatives[which][step] = moving[which][1]
    return relatives


def in_order(relative, axis, count):
    me = lax.axis_index(axis)
    order = (jnp.arange(count, dtype=jnp.int32) - me) % count
    return jnp.take(jnp.stack(relative), order, axis=0)


def per_device(
    node_features, block_mask, w_qkv, w_out, norm_gain, routes, gates, w_gate_up, w_down
):
    feats = node_features[0]
    node_dev, width = feats.shape
    seq_count = lax.axis_size("seq")
    exp_count = lax.axis_size("exp")
    experts = seq_count * exp_count * w_gate_up.shape[0]
    head_cols = w_qkv.shape[1]
    out_all = lax.all_gather(w_out[None], ("seq", "exp"), axis=0, tiled=True)
    col_pieces, chunks = ring_gather((w_qkv, feats), ("exp", "seq"), (exp_count, seq_count))
    cols_slice = in_order(col_pieces, "exp", exp_count)
    cols_slice = cols_slice.reshape(exp_count * w_qkv.shape[0], head_cols)
    projected_rel = [
        jnp.dot(chunk, cols_slice, preferred_element_type=jnp.float32).astype(jnp.bfloat16)
        for chunk in chunks
    ]
    projected = in_order(projected_rel, "seq", seq_count).reshape(seq_count * node_dev, head_cols)
    nodes = projected.shape[0]
    heads_here = head_cols // (3 * HEAD_DIM)
    split = projected.reshape(nodes, heads_here, 3, HEAD_DIM)
    query = split[:, :, 0]
    keys = split[:, :, 1]
    values = split[:, :, 2]
    col_mask = jnp.repeat(block_mask[0], BLOCK, axis=1) > 0
    span = math.gcd(nodes, 512)
    scale = 1.0 / math.sqrt(HEAD_DIM)

    def attend(index):
        start = index * span
        rows_query = lax.dynamic_slice_in_dim(query, start, span, 0)
        rows_mask = lax.dynamic_slice_in_dim(col_mask, start // BLOCK, span // BLOCK, 0)
        allowed = jnp.repeat(rows_mask, BLOCK, axis=0)
        scores = (
            jnp.einsum("qhd,khd->hqk", rows_query, keys, preferred_element_type=jnp.float32) * scale
        )
        scores = jnp.where(allowed[None], scores, -1e30)
        top = jnp.max(scores, axis=-1, keepdims=True)
        weights = jnp.exp(scores - top)
        probs = (weights / jnp.sum(weights, axis=-1, keepdims=True)).astype(jnp.bfloat16)
        return jnp.einsum("hqk,khd->qhd", probs, values, preferred_element_type=jnp.float32).astype(
            jnp.bfloat16
        )

    blocks = lax.map(attend, jnp.arange(nodes // span, dtype=jnp.int32))
    attended = blocks.reshape(nodes, heads_here * HEAD_DIM)
    node_attended = lax.all_to_all(attended, "seq", split_axis=0, concat_axis=1, tiled=True)
    out_tiles = out_all.reshape(seq_count, exp_count, w_out.shape[0], w_out.shape[1])
    attn_out = jnp.einsum(
        "nsk,sekc->nec",
        node_attended.reshape(node_dev, seq_count, w_out.shape[0]),
        out_tiles,
        preferred_element_type=jnp.float32,
    )
    mixed = feats.astype(jnp.float32) + attn_out.reshape(node_dev, width)
    mean_square = jnp.mean(mixed * mixed, axis=-1, keepdims=True)
    normed = (mixed * lax.rsqrt(mean_square + 1e-06) * norm_gain).astype(jnp.bfloat16)
    capacity = 2 * TOP * node_dev // experts
    pair_routes = routes[0].reshape(node_dev * TOP)
    onehot = (pair_routes[:, None] == jnp.arange(experts, dtype=jnp.int32)).astype(jnp.int32)
    earlier = jnp.cumsum(onehot, axis=0, dtype=jnp.int32) - onehot
    slots = jnp.sum(earlier * onehot, axis=1, dtype=jnp.int32)
    position = (pair_routes * capacity + slots).reshape(node_dev, TOP)
    places = jnp.arange(experts * capacity, dtype=jnp.int32).reshape(experts, capacity)
    select = (places[:, :, None, None] == position[None, None]).astype(jnp.bfloat16)
    outgoing = jnp.einsum(
        "ecn,nd->ecd", jnp.sum(select, axis=3), normed, preferred_element_type=jnp.float32
    ).astype(jnp.bfloat16)
    hidden_units = w_down.shape[1]
    received = lax.all_to_all(outgoing, ("seq", "exp"), split_axis=0, concat_axis=0, tiled=True)
    both = jnp.einsum("eck,kf->ecf", received, w_gate_up[0], preferred_element_type=jnp.float32)
    hidden = (jax.nn.silu(both[..., :hidden_units]) * both[..., hidden_units:]).astype(jnp.bfloat16)
    processed = jnp.einsum(
        "ecf,fd->ecd", hidden, w_down[0], preferred_element_type=jnp.float32
    ).astype(jnp.bfloat16)
    returned = lax.all_to_all(processed, ("seq", "exp"), split_axis=0, concat_axis=0, tiled=True)
    picked = jnp.einsum("ecnk,ecd->knd", select, returned, preferred_element_type=jnp.float32)
    expert_sum = picked[0] * gates[0][:, 0, None] + picked[1] * gates[0][:, 1, None]
    return (mixed + expert_sum).astype(jnp.bfloat16)[None]


def solution(mesh):
    in_specs = (
        P(("sub", "exp"), "seq", None),
        P(("sub", "exp"), None, None),
        P("exp", "seq"),
        P("seq", "exp"),
        P(),
        P(("sub", "exp"), "seq", None),
        P(("sub", "exp"), "seq", None),
        P(("seq", "exp"), None, None),
        P(("seq", "exp"), None, None),
    )
    out_specs = P(("sub", "exp"), "seq", None)
    return jax.shard_map(
        per_device, mesh=mesh, in_specs=in_specs, out_specs=out_specs, check_vma=False
    )
```

```python
import math

import jax
import jax.numpy as jnp
from jax import lax
from jax.sharding import PartitionSpec as P

HEAD_DIM = 64
TOP = 2
BLOCK = 128


def ring_gather(pieces, axes, counts):
    relatives = [[piece] + [None] * (count - 1) for piece, count in zip(pieces, counts)]
    moving = [[piece, piece] for piece in pieces]
    for step in range(1, max(counts) // 2 + 1):
        for which, (axis, count) in enumerate(zip(axes, counts)):
            if step > count // 2:
                continue
            right = [(i, (i + 1) % count) for i in range(count)]
            left = [(i, (i - 1) % count) for i in range(count)]
            moving[which][0] = lax.ppermute(moving[which][0], axis, right)
            relatives[which][(count - step) % count] = moving[which][0]
            if step < count - step:
                moving[which][1] = lax.ppermute(moving[which][1], axis, left)
                relatives[which][step] = moving[which][1]
        moving = lax.optimization_barrier(moving)
        for which, count in enumerate(counts):
            if step <= count // 2:
                relatives[which][(count - step) % count] = moving[which][0]
                if step < count - step:
                    relatives[which][step] = moving[which][1]
    return relatives


def in_order(relative, axis, count):
    me = lax.axis_index(axis)
    order = (jnp.arange(count, dtype=jnp.int32) - me) % count
    return jnp.take(jnp.stack(relative), order, axis=0)


def per_device(
    node_features, block_mask, w_qkv, w_out, norm_gain, routes, gates, w_gate_up, w_down
):
    feats = node_features[0]
    node_dev, width = feats.shape
    seq_count = lax.axis_size("seq")
    exp_count = lax.axis_size("exp")
    experts = seq_count * exp_count * w_gate_up.shape[0]
    head_cols = w_qkv.shape[1]
    out_all = lax.all_gather(w_out[None], ("seq", "exp"), axis=0, tiled=True)
    col_pieces, chunks = ring_gather((w_qkv, feats), ("exp", "seq"), (exp_count, seq_count))
    cols_slice = in_order(col_pieces, "exp", exp_count)
    cols_slice = cols_slice.reshape(exp_count * w_qkv.shape[0], head_cols)
    gathered = jnp.stack(chunks).reshape(seq_count * node_dev, width)
    projected = jnp.dot(gathered, cols_slice, preferred_element_type=jnp.float32).astype(
        jnp.bfloat16
    )
    nodes = projected.shape[0]
    heads_here = head_cols // (3 * HEAD_DIM)
    split = projected.reshape(seq_count, node_dev, heads_here, 3, HEAD_DIM)
    me = lax.axis_index("seq")
    to_node = (jnp.arange(seq_count, dtype=jnp.int32) - me) % seq_count
    to_ring = (jnp.arange(seq_count, dtype=jnp.int32) + me) % seq_count
    query = jnp.take(split[:, :, :, 0], to_node, axis=0).reshape(nodes, heads_here, HEAD_DIM)
    keys = split[:, :, :, 1].reshape(nodes, heads_here, HEAD_DIM)
    values = split[:, :, :, 2].reshape(nodes, heads_here, HEAD_DIM)
    col_mask = jnp.repeat(block_mask[0], BLOCK, axis=1) > 0
    col_mask = jnp.take(col_mask.reshape(-1, seq_count, node_dev), to_ring, axis=1)
    col_mask = col_mask.reshape(-1, nodes)
    span = math.gcd(nodes, 512)
    scale = 1.0 / math.sqrt(HEAD_DIM)

    def attend(index):
        start = index * span
        rows_query = lax.dynamic_slice_in_dim(query, start, span, 0)
        rows_mask = lax.dynamic_slice_in_dim(col_mask, start // BLOCK, span // BLOCK, 0)
        allowed = jnp.repeat(rows_mask, BLOCK, axis=0)
        scores = (
            jnp.einsum("qhd,khd->hqk", rows_query, keys, preferred_element_type=jnp.float32) * scale
        )
        scores = jnp.where(allowed[None], scores, -1e30)
        top = jnp.max(scores, axis=-1, keepdims=True)
        weights = jnp.exp(scores - top)
        probs = (weights / jnp.sum(weights, axis=-1, keepdims=True)).astype(jnp.bfloat16)
        return jnp.einsum("hqk,khd->qhd", probs, values, preferred_element_type=jnp.float32).astype(
            jnp.bfloat16
        )

    blocks = lax.map(attend, jnp.arange(nodes // span, dtype=jnp.int32))
    attended = blocks.reshape(nodes, heads_here * HEAD_DIM)
    node_attended = lax.all_to_all(attended, "seq", split_axis=0, concat_axis=1, tiled=True)
    out_tiles = out_all.reshape(seq_count, exp_count, w_out.shape[0], w_out.shape[1])
    attn_out = jnp.einsum(
        "nsk,sekc->nec",
        node_attended.reshape(node_dev, seq_count, w_out.shape[0]),
        out_tiles,
        preferred_element_type=jnp.float32,
    )
    mixed = feats.astype(jnp.float32) + attn_out.reshape(node_dev, width)
    mean_square = jnp.mean(mixed * mixed, axis=-1, keepdims=True)
    normed = (mixed * lax.rsqrt(mean_square + 1e-06) * norm_gain).astype(jnp.bfloat16)
    capacity = 2 * TOP * node_dev // experts
    pair_routes = routes[0].reshape(node_dev * TOP)
    onehot = (pair_routes[:, None] == jnp.arange(experts, dtype=jnp.int32)).astype(jnp.int32)
    earlier = jnp.cumsum(onehot, axis=0, dtype=jnp.int32) - onehot
    slots = jnp.sum(earlier * onehot, axis=1, dtype=jnp.int32)
    position = (pair_routes * capacity + slots).reshape(node_dev, TOP)
    places = jnp.arange(experts * capacity, dtype=jnp.int32).reshape(experts, capacity)
    select = (places[:, :, None, None] == position[None, None]).astype(jnp.bfloat16)
    outgoing = jnp.einsum(
        "ecn,nd->ecd", jnp.sum(select, axis=3), normed, preferred_element_type=jnp.float32
    ).astype(jnp.bfloat16)
    hidden_units = w_down.shape[1]
    received = lax.all_to_all(outgoing, ("seq", "exp"), split_axis=0, concat_axis=0, tiled=True)
    both = jnp.einsum("eck,kf->ecf", received, w_gate_up[0], preferred_element_type=jnp.float32)
    hidden = (jax.nn.silu(both[..., :hidden_units]) * both[..., hidden_units:]).astype(jnp.bfloat16)
    processed = jnp.einsum(
        "ecf,fd->ecd", hidden, w_down[0], preferred_element_type=jnp.float32
    ).astype(jnp.bfloat16)
    returned = lax.all_to_all(processed, ("seq", "exp"), split_axis=0, concat_axis=0, tiled=True)
    picked = jnp.einsum("ecnk,ecd->knd", select, returned, preferred_element_type=jnp.float32)
    expert_sum = picked[0] * gates[0][:, 0, None] + picked[1] * gates[0][:, 1, None]
    return (mixed + expert_sum).astype(jnp.bfloat16)[None]


def solution(mesh):
    in_specs = (
        P(("sub", "exp"), "seq", None),
        P(("sub", "exp"), None, None),
        P("exp", "seq"),
        P("seq", "exp"),
        P(),
        P(("sub", "exp"), "seq", None),
        P(("sub", "exp"), "seq", None),
        P(("seq", "exp"), None, None),
        P(("seq", "exp"), None, None),
    )
    out_specs = P(("sub", "exp"), "seq", None)
    return jax.shard_map(
        per_device, mesh=mesh, in_specs=in_specs, out_specs=out_specs, check_vma=False
    )
```

```python
import functools
import math

import jax
import jax.numpy as jnp
from jax import lax
from jax.experimental import pallas as pl
from jax.experimental.pallas import tpu as pltpu
from jax.sharding import PartitionSpec as P

HEAD_DIM = 64
TOP = 2
BLOCK = 128
TILE = 64


def attention_kernel(me_ref, mask_ref, proj_ref, out_ref, *, chunk, chunks, heads, blocks):
    tile = pl.program_id(0)
    me = me_ref[0]
    per_chunk = chunk // TILE
    ring_chunk = (tile // per_chunk - me + chunks) % chunks
    start = pl.multiple_of(ring_chunk * chunk + (tile % per_chunk) * TILE, TILE)
    query_block = (tile * TILE) // BLOCK
    nodes = chunk * chunks
    key_tiles = nodes // TILE
    lane_tile = lax.broadcasted_iota(jnp.int32, (1, nodes), 1) // TILE
    allowed = jnp.zeros((1, nodes), jnp.int32)
    for t in range(key_tiles):
        node = ((me + t // per_chunk) % chunks) * chunk + (t % per_chunk) * TILE
        bit = mask_ref[query_block * blocks + node // BLOCK]
        allowed = jnp.where(lane_tile == t, bit, allowed)
    allowed = allowed > 0
    rows = proj_ref[pl.ds(start, TILE), :]
    scale = 1.0 / math.sqrt(HEAD_DIM)
    for h in range(heads):
        base = h * 3 * HEAD_DIM
        q = rows[:, base:base + HEAD_DIM]
        k = proj_ref[:, base + HEAD_DIM:base + 2 * HEAD_DIM]
        v = proj_ref[:, base + 2 * HEAD_DIM:base + 3 * HEAD_DIM]
        scores = lax.dot_general(q, k, (((1,), (1,)), ((), ())), preferred_element_type=jnp.float32) * scale
        scores = jnp.where(allowed, scores, -1e30)
        top = jnp.max(scores, axis=-1, keepdims=True)
        weights = jnp.exp(scores - top)
        probs = (weights / jnp.sum(weights, axis=-1, keepdims=True)).astype(jnp.bfloat16)
        out = jnp.dot(probs, v, preferred_element_type=jnp.float32)
        out_ref[:, h * HEAD_DIM:(h + 1) * HEAD_DIM] = out.astype(out_ref.dtype)


def attention(me, mask, projected, chunk, chunks):
    nodes, cols = projected.shape
    heads = cols // (3 * HEAD_DIM)
    blocks = mask.shape[-1]
    kernel = functools.partial(attention_kernel, chunk=chunk, chunks=chunks, heads=heads, blocks=blocks)
    return pl.pallas_call(
        kernel,
        out_shape=jax.ShapeDtypeStruct((nodes, heads * HEAD_DIM), jnp.bfloat16),
        grid_spec=pltpu.PrefetchScalarGridSpec(
            num_scalar_prefetch=2,
            grid=(nodes // TILE,),
            in_specs=[pl.BlockSpec((nodes, cols), lambda t, me, mask: (0, 0))],
            out_specs=pl.BlockSpec((TILE, heads * HEAD_DIM), lambda t, me, mask: (t, 0)),
        ),
    )(me.reshape(1), mask.reshape(-1), projected)


def ring_gather(pieces, axes, counts):
    relatives = [[piece] + [None] * (count - 1) for piece, count in zip(pieces, counts)]
    moving = [[piece, piece] for piece in pieces]
    for step in range(1, max(counts) // 2 + 1):
        for which, (axis, count) in enumerate(zip(axes, counts)):
            if step > count // 2:
                continue
            right = [(i, (i + 1) % count) for i in range(count)]
            left = [(i, (i - 1) % count) for i in range(count)]
            moving[which][0] = lax.ppermute(moving[which][0], axis, right)
            relatives[which][(count - step) % count] = moving[which][0]
            if step < count - step:
                moving[which][1] = lax.ppermute(moving[which][1], axis, left)
                relatives[which][step] = moving[which][1]
        moving = lax.optimization_barrier(moving)
        for which, count in enumerate(counts):
            if step <= count // 2:
                relatives[which][(count - step) % count] = moving[which][0]
                if step < count - step:
                    relatives[which][step] = moving[which][1]
    return relatives


def in_order(relative, axis, count):
    me = lax.axis_index(axis)
    order = (jnp.arange(count, dtype=jnp.int32) - me) % count
    return jnp.take(jnp.stack(relative), order, axis=0)


def per_device(
    node_features, block_mask, w_qkv, w_out, norm_gain, routes, gates, w_gate_up, w_down
):
    feats = node_features[0]
    node_dev, width = feats.shape
    seq_count = lax.axis_size("seq")
    exp_count = lax.axis_size("exp")
    experts = seq_count * exp_count * w_gate_up.shape[0]
    head_cols = w_qkv.shape[1]
    out_all = lax.all_gather(w_out[None], ("seq", "exp"), axis=0, tiled=True)
    col_pieces, chunks = ring_gather((w_qkv, feats), ("exp", "seq"), (exp_count, seq_count))
    cols_slice = in_order(col_pieces, "exp", exp_count)
    cols_slice = cols_slice.reshape(exp_count * w_qkv.shape[0], head_cols)
    gathered = jnp.stack(chunks).reshape(seq_count * node_dev, width)
    projected = jnp.dot(gathered, cols_slice, preferred_element_type=jnp.float32).astype(
        jnp.bfloat16
    )
    me = lax.axis_index("seq").astype(jnp.int32)
    attended = attention(me, block_mask[0], projected, node_dev, seq_count)
    node_attended = lax.all_to_all(attended, "seq", split_axis=0, concat_axis=1, tiled=True)
    out_tiles = out_all.reshape(seq_count, exp_count, w_out.shape[0], w_out.shape[1])
    attn_out = jnp.einsum(
        "nsk,sekc->nec",
        node_attended.reshape(node_dev, seq_count, w_out.shape[0]),
        out_tiles,
        preferred_element_type=jnp.float32,
    )
    mixed = feats.astype(jnp.float32) + attn_out.reshape(node_dev, width)
    mean_square = jnp.mean(mixed * mixed, axis=-1, keepdims=True)
    normed = (mixed * lax.rsqrt(mean_square + 1e-06) * norm_gain).astype(jnp.bfloat16)
    capacity = 2 * TOP * node_dev // experts
    pair_routes = routes[0].reshape(node_dev * TOP)
    onehot = (pair_routes[:, None] == jnp.arange(experts, dtype=jnp.int32)).astype(jnp.int32)
    earlier = jnp.cumsum(onehot, axis=0, dtype=jnp.int32) - onehot
    slots = jnp.sum(earlier * onehot, axis=1, dtype=jnp.int32)
    position = (pair_routes * capacity + slots).reshape(node_dev, TOP)
    places = jnp.arange(experts * capacity, dtype=jnp.int32).reshape(experts, capacity)
    select = (places[:, :, None, None] == position[None, None]).astype(jnp.bfloat16)
    outgoing = jnp.einsum(
        "ecn,nd->ecd", jnp.sum(select, axis=3), normed, preferred_element_type=jnp.float32
    ).astype(jnp.bfloat16)
    hidden_units = w_down.shape[1]
    received = lax.all_to_all(outgoing, ("seq", "exp"), split_axis=0, concat_axis=0, tiled=True)
    both = jnp.einsum("eck,kf->ecf", received, w_gate_up[0], preferred_element_type=jnp.float32)
    hidden = (jax.nn.silu(both[..., :hidden_units]) * both[..., hidden_units:]).astype(jnp.bfloat16)
    processed = jnp.einsum(
        "ecf,fd->ecd", hidden, w_down[0], preferred_element_type=jnp.float32
    ).astype(jnp.bfloat16)
    returned = lax.all_to_all(processed, ("seq", "exp"), split_axis=0, concat_axis=0, tiled=True)
    picked = jnp.einsum("ecnk,ecd->knd", select, returned, preferred_element_type=jnp.float32)
    expert_sum = picked[0] * gates[0][:, 0, None] + picked[1] * gates[0][:, 1, None]
    return (mixed + expert_sum).astype(jnp.bfloat16)[None]


def solution(mesh):
    in_specs = (
        P(("sub", "exp"), "seq", None),
        P(("sub", "exp"), None, None),
        P("exp", "seq"),
        P("seq", "exp"),
        P(),
        P(("sub", "exp"), "seq", None),
        P(("sub", "exp"), "seq", None),
        P(("seq", "exp"), None, None),
        P(("seq", "exp"), None, None),
    )
    out_specs = P(("sub", "exp"), "seq", None)
    return jax.shard_map(
        per_device, mesh=mesh, in_specs=in_specs, out_specs=out_specs, check_vma=False
    )
```

```python
import functools
import math

import jax
import jax.numpy as jnp
from jax import lax
from jax.experimental import pallas as pl
from jax.experimental.pallas import tpu as pltpu
from jax.sharding import PartitionSpec as P

HEAD_DIM = 64
TOP = 2
BLOCK = 128
TILE = 64


def attention_kernel(me_ref, mask_ref, proj_ref, out_ref, *, chunk, chunks, heads, blocks):
    c = pl.program_id(0)
    me = me_ref[0]
    start = pl.multiple_of(((c - me + chunks) % chunks) * chunk, TILE)
    nodes = chunk * chunks
    per_chunk = chunk // TILE
    first = (c * chunk) // BLOCK
    split_row = (first + 1) * BLOCK - c * chunk
    lane_tile = lax.broadcasted_iota(jnp.int32, (1, nodes), 1) // TILE
    lanes_a = jnp.zeros((1, nodes), jnp.int32)
    lanes_b = jnp.zeros((1, nodes), jnp.int32)
    for t in range(nodes // TILE):
        node = ((me + t // per_chunk) % chunks) * chunk + (t % per_chunk) * TILE
        lanes_a = jnp.where(lane_tile == t, mask_ref[first * blocks + node // BLOCK], lanes_a)
        second = jnp.minimum(first + 1, blocks - 1)
        lanes_b = jnp.where(lane_tile == t, mask_ref[second * blocks + node // BLOCK], lanes_b)
    row = lax.broadcasted_iota(jnp.int32, (chunk, 1), 0)
    allowed = jnp.where(row < split_row, lanes_a, lanes_b) > 0
    rows = proj_ref[pl.ds(start, chunk), :]
    scale = 1.0 / math.sqrt(HEAD_DIM)
    for h in range(heads):
        base = h * 3 * HEAD_DIM
        q = rows[:, base:base + HEAD_DIM]
        k = proj_ref[:, base + HEAD_DIM:base + 2 * HEAD_DIM]
        v = proj_ref[:, base + 2 * HEAD_DIM:base + 3 * HEAD_DIM]
        scores = lax.dot_general(q, k, (((1,), (1,)), ((), ())), preferred_element_type=jnp.float32) * scale
        scores = jnp.where(allowed, scores, -1e30)
        top = jnp.max(scores, axis=-1, keepdims=True)
        weights = jnp.exp(scores - top)
        inverse = 1.0 / jnp.sum(weights, axis=-1, keepdims=True)
        probs = (weights * inverse).astype(jnp.bfloat16)
        out = jnp.dot(probs, v, preferred_element_type=jnp.float32)
        out_ref[:, h * HEAD_DIM:(h + 1) * HEAD_DIM] = out.astype(out_ref.dtype)


def attention(me, mask, projected, chunk, chunks):
    nodes, cols = projected.shape
    heads = cols // (3 * HEAD_DIM)
    blocks = mask.shape[-1]
    kernel = functools.partial(attention_kernel, chunk=chunk, chunks=chunks, heads=heads, blocks=blocks)
    return pl.pallas_call(
        kernel,
        out_shape=jax.ShapeDtypeStruct((nodes, heads * HEAD_DIM), jnp.bfloat16),
        grid_spec=pltpu.PrefetchScalarGridSpec(
            num_scalar_prefetch=2,
            grid=(chunks,),
            in_specs=[pl.BlockSpec((nodes, cols), lambda c, me, mask: (0, 0))],
            out_specs=pl.BlockSpec((chunk, heads * HEAD_DIM), lambda c, me, mask: (c, 0)),
        ),
    )(me.reshape(1), mask.reshape(-1), projected)


def ring_gather(pieces, axes, counts):
    relatives = [[piece] + [None] * (count - 1) for piece, count in zip(pieces, counts)]
    moving = [[piece, piece] for piece in pieces]
    for step in range(1, max(counts) // 2 + 1):
        for which, (axis, count) in enumerate(zip(axes, counts)):
            if step > count // 2:
                continue
            right = [(i, (i + 1) % count) for i in range(count)]
            left = [(i, (i - 1) % count) for i in range(count)]
            moving[which][0] = lax.ppermute(moving[which][0], axis, right)
            relatives[which][(count - step) % count] = moving[which][0]
            if step < count - step:
                moving[which][1] = lax.ppermute(moving[which][1], axis, left)
                relatives[which][step] = moving[which][1]
        moving = lax.optimization_barrier(moving)
        for which, count in enumerate(counts):
            if step <= count // 2:
                relatives[which][(count - step) % count] = moving[which][0]
                if step < count - step:
                    relatives[which][step] = moving[which][1]
    return relatives


def in_order(relative, axis, count):
    me = lax.axis_index(axis)
    order = (jnp.arange(count, dtype=jnp.int32) - me) % count
    return jnp.take(jnp.stack(relative), order, axis=0)


def per_device(
    node_features, block_mask, w_qkv, w_out, norm_gain, routes, gates, w_gate_up, w_down
):
    feats = node_features[0]
    node_dev, width = feats.shape
    seq_count = lax.axis_size("seq")
    exp_count = lax.axis_size("exp")
    experts = seq_count * exp_count * w_gate_up.shape[0]
    head_cols = w_qkv.shape[1]
    out_all = lax.all_gather(w_out[None], ("seq", "exp"), axis=0, tiled=True)
    col_pieces, chunks = ring_gather((w_qkv, feats), ("exp", "seq"), (exp_count, seq_count))
    cols_slice = in_order(col_pieces, "exp", exp_count)
    cols_slice = cols_slice.reshape(exp_count * w_qkv.shape[0], head_cols)
    gathered = jnp.stack(chunks).reshape(seq_count * node_dev, width)
    projected = jnp.dot(gathered, cols_slice, preferred_element_type=jnp.float32).astype(
        jnp.bfloat16
    )
    me = lax.axis_index("seq").astype(jnp.int32)
    attended = attention(me, block_mask[0], projected, node_dev, seq_count)
    node_attended = lax.all_to_all(attended, "seq", split_axis=0, concat_axis=1, tiled=True)
    out_tiles = out_all.reshape(seq_count, exp_count, w_out.shape[0], w_out.shape[1])
    attn_out = jnp.einsum(
        "nsk,sekc->nec",
        node_attended.reshape(node_dev, seq_count, w_out.shape[0]),
        out_tiles,
        preferred_element_type=jnp.float32,
    )
    mixed = feats.astype(jnp.float32) + attn_out.reshape(node_dev, width)
    mean_square = jnp.mean(mixed * mixed, axis=-1, keepdims=True)
    normed = (mixed * lax.rsqrt(mean_square + 1e-06) * norm_gain).astype(jnp.bfloat16)
    capacity = 2 * TOP * node_dev // experts
    pair_routes = routes[0].reshape(node_dev * TOP)
    onehot = (pair_routes[:, None] == jnp.arange(experts, dtype=jnp.int32)).astype(jnp.int32)
    earlier = jnp.cumsum(onehot, axis=0, dtype=jnp.int32) - onehot
    slots = jnp.sum(earlier * onehot, axis=1, dtype=jnp.int32)
    position = (pair_routes * capacity + slots).reshape(node_dev, TOP)
    places = jnp.arange(experts * capacity, dtype=jnp.int32).reshape(experts, capacity)
    select = (places[:, :, None, None] == position[None, None]).astype(jnp.bfloat16)
    outgoing = jnp.einsum(
        "ecn,nd->ecd", jnp.sum(select, axis=3), normed, preferred_element_type=jnp.float32
    ).astype(jnp.bfloat16)
    hidden_units = w_down.shape[1]
    received = lax.all_to_all(outgoing, ("seq", "exp"), split_axis=0, concat_axis=0, tiled=True)
    both = jnp.einsum("eck,kf->ecf", received, w_gate_up[0], preferred_element_type=jnp.float32)
    hidden = (jax.nn.silu(both[..., :hidden_units]) * both[..., hidden_units:]).astype(jnp.bfloat16)
    processed = jnp.einsum(
        "ecf,fd->ecd", hidden, w_down[0], preferred_element_type=jnp.float32
    ).astype(jnp.bfloat16)
    returned = lax.all_to_all(processed, ("seq", "exp"), split_axis=0, concat_axis=0, tiled=True)
    picked = jnp.einsum("ecnk,ecd->knd", select, returned, preferred_element_type=jnp.float32)
    expert_sum = picked[0] * gates[0][:, 0, None] + picked[1] * gates[0][:, 1, None]
    return (mixed + expert_sum).astype(jnp.bfloat16)[None]


def solution(mesh):
    in_specs = (
        P(("sub", "exp"), "seq", None),
        P(("sub", "exp"), None, None),
        P("exp", "seq"),
        P("seq", "exp"),
        P(),
        P(("sub", "exp"), "seq", None),
        P(("sub", "exp"), "seq", None),
        P(("seq", "exp"), None, None),
        P(("seq", "exp"), None, None),
    )
    out_specs = P(("sub", "exp"), "seq", None)
    return jax.shard_map(
        per_device, mesh=mesh, in_specs=in_specs, out_specs=out_specs, check_vma=False
    )
```

```python
import functools
import math

import jax
import jax.numpy as jnp
from jax import lax
from jax.experimental import pallas as pl
from jax.experimental.pallas import tpu as pltpu
from jax.sharding import PartitionSpec as P

HEAD_DIM = 64
TOP = 2
BLOCK = 128
TILE = 64


def attention_kernel(me_ref, mask_ref, proj_ref, out_ref, keys_t, *, chunk, chunks, heads, blocks):
    c = pl.program_id(0)
    me = me_ref[0]
    start = pl.multiple_of(((c - me + chunks) % chunks) * chunk, TILE)
    nodes = chunk * chunks
    per_chunk = chunk // TILE
    first = (c * chunk) // BLOCK
    split_row = (first + 1) * BLOCK - c * chunk
    lane_tile = lax.broadcasted_iota(jnp.int32, (1, nodes), 1) // TILE
    lanes_a = jnp.zeros((1, nodes), jnp.int32)
    lanes_b = jnp.zeros((1, nodes), jnp.int32)
    for t in range(nodes // TILE):
        node = ((me + t // per_chunk) % chunks) * chunk + (t % per_chunk) * TILE
        lanes_a = jnp.where(lane_tile == t, mask_ref[first * blocks + node // BLOCK], lanes_a)
        second = jnp.minimum(first + 1, blocks - 1)
        lanes_b = jnp.where(lane_tile == t, mask_ref[second * blocks + node // BLOCK], lanes_b)
    row = lax.broadcasted_iota(jnp.int32, (chunk, 1), 0)
    allowed = jnp.where(row < split_row, lanes_a, lanes_b) > 0
    rows = proj_ref[pl.ds(start, chunk), :]
    scale = 1.0 / math.sqrt(HEAD_DIM)

    @pl.when(c == 0)
    def _():
        for h in range(heads):
            base = h * 3 * HEAD_DIM
            keys_t[h] = proj_ref[:, base + HEAD_DIM:base + 2 * HEAD_DIM].T

    for h in range(heads):
        base = h * 3 * HEAD_DIM
        q = rows[:, base:base + HEAD_DIM]
        v = proj_ref[:, base + 2 * HEAD_DIM:base + 3 * HEAD_DIM]
        scores = jnp.dot(q, keys_t[h], preferred_element_type=jnp.float32) * scale
        scores = jnp.where(allowed, scores, -1e30)
        top = jnp.max(scores, axis=-1, keepdims=True)
        weights = jnp.exp(scores - top)
        inverse = 1.0 / jnp.sum(weights, axis=-1, keepdims=True)
        probs = (weights * inverse).astype(jnp.bfloat16)
        out = jnp.dot(probs, v, preferred_element_type=jnp.float32)
        out_ref[:, h * HEAD_DIM:(h + 1) * HEAD_DIM] = out.astype(out_ref.dtype)


def attention(me, mask, projected, chunk, chunks):
    nodes, cols = projected.shape
    heads = cols // (3 * HEAD_DIM)
    blocks = mask.shape[-1]
    kernel = functools.partial(attention_kernel, chunk=chunk, chunks=chunks, heads=heads, blocks=blocks)
    return pl.pallas_call(
        kernel,
        out_shape=jax.ShapeDtypeStruct((nodes, heads * HEAD_DIM), jnp.bfloat16),
        grid_spec=pltpu.PrefetchScalarGridSpec(
            num_scalar_prefetch=2,
            grid=(chunks,),
            in_specs=[pl.BlockSpec((nodes, cols), lambda c, me, mask: (0, 0))],
            out_specs=pl.BlockSpec((chunk, heads * HEAD_DIM), lambda c, me, mask: (c, 0)),
            scratch_shapes=[pltpu.VMEM((heads, HEAD_DIM, nodes), jnp.bfloat16)],
        ),
    )(me.reshape(1), mask.reshape(-1), projected)


def ring_gather(pieces, axes, counts):
    relatives = [[piece] + [None] * (count - 1) for piece, count in zip(pieces, counts)]
    moving = [[piece, piece] for piece in pieces]
    for step in range(1, max(counts) // 2 + 1):
        for which, (axis, count) in enumerate(zip(axes, counts)):
            if step > count // 2:
                continue
            right = [(i, (i + 1) % count) for i in range(count)]
            left = [(i, (i - 1) % count) for i in range(count)]
            moving[which][0] = lax.ppermute(moving[which][0], axis, right)
            relatives[which][(count - step) % count] = moving[which][0]
            if step < count - step:
                moving[which][1] = lax.ppermute(moving[which][1], axis, left)
                relatives[which][step] = moving[which][1]
        moving = lax.optimization_barrier(moving)
        for which, count in enumerate(counts):
            if step <= count // 2:
                relatives[which][(count - step) % count] = moving[which][0]
                if step < count - step:
                    relatives[which][step] = moving[which][1]
    return relatives


def in_order(relative, axis, count):
    me = lax.axis_index(axis)
    order = (jnp.arange(count, dtype=jnp.int32) - me) % count
    return jnp.take(jnp.stack(relative), order, axis=0)


def per_device(
    node_features, block_mask, w_qkv, w_out, norm_gain, routes, gates, w_gate_up, w_down
):
    feats = node_features[0]
    node_dev, width = feats.shape
    seq_count = lax.axis_size("seq")
    exp_count = lax.axis_size("exp")
    experts = seq_count * exp_count * w_gate_up.shape[0]
    head_cols = w_qkv.shape[1]
    out_all = lax.all_gather(w_out[None], ("seq", "exp"), axis=0, tiled=True)
    col_pieces, chunks = ring_gather((w_qkv, feats), ("exp", "seq"), (exp_count, seq_count))
    cols_slice = in_order(col_pieces, "exp", exp_count)
    cols_slice = cols_slice.reshape(exp_count * w_qkv.shape[0], head_cols)
    gathered = jnp.stack(chunks).reshape(seq_count * node_dev, width)
    projected = jnp.dot(gathered, cols_slice, preferred_element_type=jnp.float32).astype(
        jnp.bfloat16
    )
    me = lax.axis_index("seq").astype(jnp.int32)
    attended = attention(me, block_mask[0], projected, node_dev, seq_count)
    node_attended = lax.all_to_all(attended, "seq", split_axis=0, concat_axis=1, tiled=True)
    out_tiles = out_all.reshape(seq_count, exp_count, w_out.shape[0], w_out.shape[1])
    attn_out = jnp.einsum(
        "nsk,sekc->nec",
        node_attended.reshape(node_dev, seq_count, w_out.shape[0]),
        out_tiles,
        preferred_element_type=jnp.float32,
    )
    mixed = feats.astype(jnp.float32) + attn_out.reshape(node_dev, width)
    mean_square = jnp.mean(mixed * mixed, axis=-1, keepdims=True)
    normed = (mixed * lax.rsqrt(mean_square + 1e-06) * norm_gain).astype(jnp.bfloat16)
    capacity = 2 * TOP * node_dev // experts
    pair_routes = routes[0].reshape(node_dev * TOP)
    onehot = (pair_routes[:, None] == jnp.arange(experts, dtype=jnp.int32)).astype(jnp.int32)
    earlier = jnp.cumsum(onehot, axis=0, dtype=jnp.int32) - onehot
    slots = jnp.sum(earlier * onehot, axis=1, dtype=jnp.int32)
    position = (pair_routes * capacity + slots).reshape(node_dev, TOP)
    places = jnp.arange(experts * capacity, dtype=jnp.int32).reshape(experts, capacity)
    select = (places[:, :, None, None] == position[None, None]).astype(jnp.bfloat16)
    outgoing = jnp.einsum(
        "ecn,nd->ecd", jnp.sum(select, axis=3), normed, preferred_element_type=jnp.float32
    ).astype(jnp.bfloat16)
    hidden_units = w_down.shape[1]
    received = lax.all_to_all(outgoing, ("seq", "exp"), split_axis=0, concat_axis=0, tiled=True)
    both = jnp.einsum("eck,kf->ecf", received, w_gate_up[0], preferred_element_type=jnp.float32)
    hidden = (jax.nn.silu(both[..., :hidden_units]) * both[..., hidden_units:]).astype(jnp.bfloat16)
    processed = jnp.einsum(
        "ecf,fd->ecd", hidden, w_down[0], preferred_element_type=jnp.float32
    ).astype(jnp.bfloat16)
    returned = lax.all_to_all(processed, ("seq", "exp"), split_axis=0, concat_axis=0, tiled=True)
    picked = jnp.einsum("ecnk,ecd->knd", select, returned, preferred_element_type=jnp.float32)
    expert_sum = picked[0] * gates[0][:, 0, None] + picked[1] * gates[0][:, 1, None]
    return (mixed + expert_sum).astype(jnp.bfloat16)[None]


def solution(mesh):
    in_specs = (
        P(("sub", "exp"), "seq", None),
        P(("sub", "exp"), None, None),
        P("exp", "seq"),
        P("seq", "exp"),
        P(),
        P(("sub", "exp"), "seq", None),
        P(("sub", "exp"), "seq", None),
        P(("seq", "exp"), None, None),
        P(("seq", "exp"), None, None),
    )
    out_specs = P(("sub", "exp"), "seq", None)
    return jax.shard_map(
        per_device, mesh=mesh, in_specs=in_specs, out_specs=out_specs, check_vma=False
    )
```

```python
import functools
import math

import jax
import jax.numpy as jnp
from jax import lax
from jax.experimental import pallas as pl
from jax.experimental.pallas import tpu as pltpu
from jax.sharding import PartitionSpec as P

HEAD_DIM = 64
TOP = 2
BLOCK = 128
TILE = 64


def attention_kernel(
    me_ref, mask_ref, *refs, chunk, chunks, heads, blocks, width, pieces, piece_rows
):
    chunk_refs = refs[:chunks]
    w_ref, out_ref, proj, w_rows, keys_t = refs[chunks:]
    c = pl.program_id(0)
    me = me_ref[0]
    nodes = chunk * chunks

    @pl.when(c == 0)
    def _():
        for b in range(pieces):
            w_rows[b * piece_rows:(b + 1) * piece_rows, :] = w_ref[(b - me_ref[1] + pieces) % pieces]
        for j in range(chunks):
            proj[j * chunk:(j + 1) * chunk, :] = jnp.dot(
                chunk_refs[j][...], w_rows[...], preferred_element_type=jnp.float32
            ).astype(proj.dtype)
        for h in range(heads):
            base = h * 3 * HEAD_DIM
            keys_t[h] = proj[:, base + HEAD_DIM:base + 2 * HEAD_DIM].T

    start = pl.multiple_of(((c - me + chunks) % chunks) * chunk, TILE)
    per_chunk = chunk // TILE
    first = (c * chunk) // BLOCK
    split_row = (first + 1) * BLOCK - c * chunk
    lane_tile = lax.broadcasted_iota(jnp.int32, (1, nodes), 1) // TILE
    lanes_a = jnp.zeros((1, nodes), jnp.int32)
    lanes_b = jnp.zeros((1, nodes), jnp.int32)
    second = jnp.minimum(first + 1, blocks - 1)
    for t in range(nodes // TILE):
        node = ((me + t // per_chunk) % chunks) * chunk + (t % per_chunk) * TILE
        lanes_a = jnp.where(lane_tile == t, mask_ref[first * blocks + node // BLOCK], lanes_a)
        lanes_b = jnp.where(lane_tile == t, mask_ref[second * blocks + node // BLOCK], lanes_b)
    row = lax.broadcasted_iota(jnp.int32, (chunk, 1), 0)
    allowed = jnp.where(row < split_row, lanes_a, lanes_b) > 0
    rows = proj[pl.ds(start, chunk), :]
    scale = 1.0 / math.sqrt(HEAD_DIM)
    for h in range(heads):
        base = h * 3 * HEAD_DIM
        q = rows[:, base:base + HEAD_DIM]
        v = proj[:, base + 2 * HEAD_DIM:base + 3 * HEAD_DIM]
        scores = jnp.dot(q, keys_t[h], preferred_element_type=jnp.float32) * scale
        scores = jnp.where(allowed, scores, -1e30)
        top = jnp.max(scores, axis=-1, keepdims=True)
        weights = jnp.exp(scores - top)
        inverse = 1.0 / jnp.sum(weights, axis=-1, keepdims=True)
        probs = (weights * inverse).astype(jnp.bfloat16)
        out = jnp.dot(probs, v, preferred_element_type=jnp.float32)
        out_ref[:, h * HEAD_DIM:(h + 1) * HEAD_DIM] = out.astype(out_ref.dtype)


def attention(me, mask, chunk_list, w_stack):
    chunks = len(chunk_list)
    chunk, width = chunk_list[0].shape
    pieces, piece_rows, cols = w_stack.shape
    nodes = chunk * chunks
    heads = cols // (3 * HEAD_DIM)
    blocks = mask.shape[-1]
    kernel = functools.partial(
        attention_kernel, chunk=chunk, chunks=chunks, heads=heads, blocks=blocks, width=width,
        pieces=pieces, piece_rows=piece_rows,
    )
    whole = lambda c, me, mask: (0, 0)
    return pl.pallas_call(
        kernel,
        out_shape=jax.ShapeDtypeStruct((nodes, heads * HEAD_DIM), jnp.bfloat16),
        grid_spec=pltpu.PrefetchScalarGridSpec(
            num_scalar_prefetch=2,
            grid=(chunks,),
            in_specs=[pl.BlockSpec((chunk, width), whole)] * chunks
            + [pl.BlockSpec((pieces, piece_rows, cols), lambda c, me, mask: (0, 0, 0))],
            out_specs=pl.BlockSpec((chunk, heads * HEAD_DIM), lambda c, me, mask: (c, 0)),
            scratch_shapes=[
                pltpu.VMEM((nodes, cols), jnp.bfloat16),
                pltpu.VMEM((pieces * piece_rows, cols), jnp.bfloat16),
                pltpu.VMEM((heads, HEAD_DIM, nodes), jnp.bfloat16),
            ],
        ),
    )(me, mask.reshape(-1), *chunk_list, w_stack)


def ring_gather(pieces, axes, counts):
    relatives = [[piece] + [None] * (count - 1) for piece, count in zip(pieces, counts)]
    moving = [[piece, piece] for piece in pieces]
    for step in range(1, max(counts) // 2 + 1):
        for which, (axis, count) in enumerate(zip(axes, counts)):
            if step > count // 2:
                continue
            right = [(i, (i + 1) % count) for i in range(count)]
            left = [(i, (i - 1) % count) for i in range(count)]
            moving[which][0] = lax.ppermute(moving[which][0], axis, right)
            relatives[which][(count - step) % count] = moving[which][0]
            if step < count - step:
                moving[which][1] = lax.ppermute(moving[which][1], axis, left)
                relatives[which][step] = moving[which][1]
        moving = lax.optimization_barrier(moving)
        for which, count in enumerate(counts):
            if step <= count // 2:
                relatives[which][(count - step) % count] = moving[which][0]
                if step < count - step:
                    relatives[which][step] = moving[which][1]
    return relatives


def per_device(
    node_features, block_mask, w_qkv, w_out, norm_gain, routes, gates, w_gate_up, w_down
):
    feats = node_features[0]
    node_dev, width = feats.shape
    seq_count = lax.axis_size("seq")
    exp_count = lax.axis_size("exp")
    experts = seq_count * exp_count * w_gate_up.shape[0]
    head_cols = w_qkv.shape[1]
    out_all = lax.all_gather(w_out[None], ("seq", "exp"), axis=0, tiled=True)
    col_pieces, chunks = ring_gather((w_qkv, feats), ("exp", "seq"), (exp_count, seq_count))
    me = jnp.stack([lax.axis_index("seq"), lax.axis_index("exp")]).astype(jnp.int32)
    attended = attention(me, block_mask[0], chunks, jnp.stack(col_pieces))
    node_attended = lax.all_to_all(attended, "seq", split_axis=0, concat_axis=1, tiled=True)
    out_tiles = out_all.reshape(seq_count, exp_count, w_out.shape[0], w_out.shape[1])
    attn_out = jnp.einsum(
        "nsk,sekc->nec",
        node_attended.reshape(node_dev, seq_count, w_out.shape[0]),
        out_tiles,
        preferred_element_type=jnp.float32,
    )
    mixed = feats.astype(jnp.float32) + attn_out.reshape(node_dev, width)
    mean_square = jnp.mean(mixed * mixed, axis=-1, keepdims=True)
    normed = (mixed * lax.rsqrt(mean_square + 1e-06) * norm_gain).astype(jnp.bfloat16)
    capacity = 2 * TOP * node_dev // experts
    pair_routes = routes[0].reshape(node_dev * TOP)
    onehot = (pair_routes[:, None] == jnp.arange(experts, dtype=jnp.int32)).astype(jnp.int32)
    earlier = jnp.cumsum(onehot, axis=0, dtype=jnp.int32) - onehot
    slots = jnp.sum(earlier * onehot, axis=1, dtype=jnp.int32)
    position = (pair_routes * capacity + slots).reshape(node_dev, TOP)
    places = jnp.arange(experts * capacity, dtype=jnp.int32).reshape(experts, capacity)
    select = (places[:, :, None, None] == position[None, None]).astype(jnp.bfloat16)
    outgoing = jnp.einsum(
        "ecn,nd->ecd", jnp.sum(select, axis=3), normed, preferred_element_type=jnp.float32
    ).astype(jnp.bfloat16)
    hidden_units = w_down.shape[1]
    received = lax.all_to_all(outgoing, ("seq", "exp"), split_axis=0, concat_axis=0, tiled=True)
    both = jnp.einsum("eck,kf->ecf", received, w_gate_up[0], preferred_element_type=jnp.float32)
    hidden = (jax.nn.silu(both[..., :hidden_units]) * both[..., hidden_units:]).astype(jnp.bfloat16)
    processed = jnp.einsum(
        "ecf,fd->ecd", hidden, w_down[0], preferred_element_type=jnp.float32
    ).astype(jnp.bfloat16)
    returned = lax.all_to_all(processed, ("seq", "exp"), split_axis=0, concat_axis=0, tiled=True)
    picked = jnp.einsum("ecnk,ecd->knd", select, returned, preferred_element_type=jnp.float32)
    expert_sum = picked[0] * gates[0][:, 0, None] + picked[1] * gates[0][:, 1, None]
    return (mixed + expert_sum).astype(jnp.bfloat16)[None]


def solution(mesh):
    in_specs = (
        P(("sub", "exp"), "seq", None),
        P(("sub", "exp"), None, None),
        P("exp", "seq"),
        P("seq", "exp"),
        P(),
        P(("sub", "exp"), "seq", None),
        P(("sub", "exp"), "seq", None),
        P(("seq", "exp"), None, None),
        P(("seq", "exp"), None, None),
    )
    out_specs = P(("sub", "exp"), "seq", None)
    return jax.shard_map(
        per_device, mesh=mesh, in_specs=in_specs, out_specs=out_specs, check_vma=False
    )
```

```python
import functools
import math

import jax
import jax.numpy as jnp
from jax import lax
from jax.experimental import pallas as pl
from jax.experimental.pallas import tpu as pltpu
from jax.sharding import PartitionSpec as P

HEAD_DIM = 64
TOP = 2
BLOCK = 128
TILE = 64


def attention_kernel(
    me_ref, mask_ref, *refs, chunk, chunks, heads, blocks, width, pieces, piece_rows
):
    chunk_refs = refs[:chunks]
    w_ref, out_ref, proj, w_rows, keys_t = refs[chunks:]
    c = pl.program_id(0)
    me = me_ref[0]
    nodes = chunk * chunks

    @pl.when(c == 0)
    def _():
        for b in range(pieces):
            w_rows[b * piece_rows:(b + 1) * piece_rows, :] = w_ref[(b - me_ref[1] + pieces) % pieces]
        for j in range(chunks):
            proj[j * chunk:(j + 1) * chunk, :] = jnp.dot(
                chunk_refs[j][...], w_rows[...], preferred_element_type=jnp.float32
            ).astype(proj.dtype)
        for h in range(heads):
            base = h * 3 * HEAD_DIM
            keys_t[h] = proj[:, base + HEAD_DIM:base + 2 * HEAD_DIM].T

    start = pl.multiple_of(((c - me + chunks) % chunks) * chunk, TILE)
    per_chunk = chunk // TILE
    first = (c * chunk) // BLOCK
    split_row = (first + 1) * BLOCK - c * chunk
    lane_tile = lax.broadcasted_iota(jnp.int32, (1, nodes), 1) // TILE
    lanes_a = jnp.zeros((1, nodes), jnp.int32)
    lanes_b = jnp.zeros((1, nodes), jnp.int32)
    second = jnp.minimum(first + 1, blocks - 1)
    for t in range(nodes // TILE):
        node = ((me + t // per_chunk) % chunks) * chunk + (t % per_chunk) * TILE
        lanes_a = jnp.where(lane_tile == t, mask_ref[first * blocks + node // BLOCK], lanes_a)
        lanes_b = jnp.where(lane_tile == t, mask_ref[second * blocks + node // BLOCK], lanes_b)
    row = lax.broadcasted_iota(jnp.int32, (chunk, 1), 0)
    allowed = jnp.where(row < split_row, lanes_a, lanes_b) > 0
    rows = proj[pl.ds(start, chunk), :]
    scale = 1.0 / math.sqrt(HEAD_DIM)
    for h in range(heads):
        base = h * 3 * HEAD_DIM
        q = rows[:, base:base + HEAD_DIM]
        v = proj[:, base + 2 * HEAD_DIM:base + 3 * HEAD_DIM]
        scores = jnp.dot(q, keys_t[h], preferred_element_type=jnp.float32) * scale
        scores = jnp.where(allowed, scores, -1e30)
        top = jnp.max(scores, axis=-1, keepdims=True)
        weights = jnp.exp(scores - top)
        inverse = 1.0 / jnp.sum(weights, axis=-1, keepdims=True)
        probs = (weights * inverse).astype(jnp.bfloat16)
        out = jnp.dot(probs, v, preferred_element_type=jnp.float32)
        out_ref[:, h * HEAD_DIM:(h + 1) * HEAD_DIM] = out.astype(out_ref.dtype)


def attention(me, mask, chunk_list, w_stack):
    chunks = len(chunk_list)
    chunk, width = chunk_list[0].shape
    pieces, piece_rows, cols = w_stack.shape
    nodes = chunk * chunks
    heads = cols // (3 * HEAD_DIM)
    blocks = mask.shape[-1]
    kernel = functools.partial(
        attention_kernel, chunk=chunk, chunks=chunks, heads=heads, blocks=blocks, width=width,
        pieces=pieces, piece_rows=piece_rows,
    )
    whole = lambda c, me, mask: (0, 0)
    return pl.pallas_call(
        kernel,
        out_shape=jax.ShapeDtypeStruct((nodes, heads * HEAD_DIM), jnp.bfloat16),
        grid_spec=pltpu.PrefetchScalarGridSpec(
            num_scalar_prefetch=2,
            grid=(chunks,),
            in_specs=[pl.BlockSpec((chunk, width), whole)] * chunks
            + [pl.BlockSpec((pieces, piece_rows, cols), lambda c, me, mask: (0, 0, 0))],
            out_specs=pl.BlockSpec((chunk, heads * HEAD_DIM), lambda c, me, mask: (c, 0)),
            scratch_shapes=[
                pltpu.VMEM((nodes, cols), jnp.bfloat16),
                pltpu.VMEM((pieces * piece_rows, cols), jnp.bfloat16),
                pltpu.VMEM((heads, HEAD_DIM, nodes), jnp.bfloat16),
            ],
        ),
    )(me, mask.reshape(-1), *chunk_list, w_stack)


def ring_gather(pieces, axes, counts):
    relatives = [[piece] + [None] * (count - 1) for piece, count in zip(pieces, counts)]
    moving = [[piece, piece] for piece in pieces]
    for step in range(1, max(counts) // 2 + 1):
        for which, (axis, count) in enumerate(zip(axes, counts)):
            if step > count // 2:
                continue
            right = [(i, (i + 1) % count) for i in range(count)]
            left = [(i, (i - 1) % count) for i in range(count)]
            moving[which][0] = lax.ppermute(moving[which][0], axis, right)
            relatives[which][(count - step) % count] = moving[which][0]
            if step < count - step:
                moving[which][1] = lax.ppermute(moving[which][1], axis, left)
                relatives[which][step] = moving[which][1]
        moving = lax.optimization_barrier(moving)
        for which, count in enumerate(counts):
            if step <= count // 2:
                relatives[which][(count - step) % count] = moving[which][0]
                if step < count - step:
                    relatives[which][step] = moving[which][1]
    return relatives


def per_device(
    node_features, block_mask, w_qkv, w_out, norm_gain, routes, gates, w_gate_up, w_down
):
    feats = node_features[0]
    node_dev, width = feats.shape
    seq_count = lax.axis_size("seq")
    exp_count = lax.axis_size("exp")
    experts = seq_count * exp_count * w_gate_up.shape[0]
    head_cols = w_qkv.shape[1]
    out_all = lax.all_gather(w_out[None], ("seq", "exp"), axis=0, tiled=True)
    col_pieces, chunks = ring_gather((w_qkv, feats), ("exp", "seq"), (exp_count, seq_count))
    me = jnp.stack([lax.axis_index("seq"), lax.axis_index("exp")]).astype(jnp.int32)
    attended = attention(me, block_mask[0], chunks, jnp.stack(col_pieces))
    node_attended = lax.all_to_all(attended, "seq", split_axis=0, concat_axis=1, tiled=True)
    out_tiles = out_all.reshape(seq_count, exp_count, w_out.shape[0], w_out.shape[1])
    attn_out = jnp.einsum(
        "nsk,sekc->nec",
        node_attended.reshape(node_dev, seq_count, w_out.shape[0]),
        out_tiles,
        preferred_element_type=jnp.float32,
    )
    mixed = feats.astype(jnp.float32) + attn_out.reshape(node_dev, width)
    mean_square = jnp.mean(mixed * mixed, axis=-1, keepdims=True)
    normed = (mixed * lax.rsqrt(mean_square + 1e-06) * norm_gain).astype(jnp.bfloat16)
    capacity = 2 * TOP * node_dev // experts
    pair_routes = routes[0].reshape(node_dev * TOP)
    onehot = (pair_routes[:, None] == jnp.arange(experts, dtype=jnp.int32)).astype(jnp.int32)
    earlier = jnp.cumsum(onehot, axis=0, dtype=jnp.int32) - onehot
    slots = jnp.sum(earlier * onehot, axis=1, dtype=jnp.int32)
    position = (pair_routes * capacity + slots).reshape(node_dev, TOP)
    places = jnp.arange(experts * capacity, dtype=jnp.int32).reshape(experts, capacity)
    select = (places[:, :, None, None] == position[None, None]).astype(jnp.bfloat16)
    outgoing = jnp.einsum(
        "ecn,nd->ecd", jnp.sum(select, axis=3), normed, preferred_element_type=jnp.float32
    ).astype(jnp.bfloat16)
    hidden_units = w_down.shape[1]
    lanes = 128
    packed = (experts, capacity * width // lanes, lanes)
    received = lax.all_to_all(
        outgoing.reshape(packed), ("seq", "exp"), split_axis=0, concat_axis=0, tiled=True
    ).reshape(experts * capacity, width)
    both = jnp.dot(received, w_gate_up[0], preferred_element_type=jnp.float32)
    hidden = (jax.nn.silu(both[:, :hidden_units]) * both[:, hidden_units:]).astype(jnp.bfloat16)
    processed = jnp.dot(hidden, w_down[0], preferred_element_type=jnp.float32).astype(jnp.bfloat16)
    returned = lax.all_to_all(
        processed.reshape(packed), ("seq", "exp"), split_axis=0, concat_axis=0, tiled=True
    ).reshape(experts, capacity, width)
    picked = jnp.einsum("ecnk,ecd->knd", select, returned, preferred_element_type=jnp.float32)
    expert_sum = picked[0] * gates[0][:, 0, None] + picked[1] * gates[0][:, 1, None]
    return (mixed + expert_sum).astype(jnp.bfloat16)[None]


def solution(mesh):
    in_specs = (
        P(("sub", "exp"), "seq", None),
        P(("sub", "exp"), None, None),
        P("exp", "seq"),
        P("seq", "exp"),
        P(),
        P(("sub", "exp"), "seq", None),
        P(("sub", "exp"), "seq", None),
        P(("seq", "exp"), None, None),
        P(("seq", "exp"), None, None),
    )
    out_specs = P(("sub", "exp"), "seq", None)
    return jax.shard_map(
        per_device, mesh=mesh, in_specs=in_specs, out_specs=out_specs, check_vma=False
    )
```

```python
import functools
import math

import jax
import jax.numpy as jnp
from jax import lax
from jax.experimental import pallas as pl
from jax.experimental.pallas import tpu as pltpu
from jax.sharding import PartitionSpec as P

HEAD_DIM = 64
TOP = 2
BLOCK = 128
TILE = 64


def attention_kernel(
    me_ref, mask_ref, *refs, chunk, chunks, heads, blocks, width, pieces, piece_rows
):
    chunk_refs = refs[:chunks]
    w_ref, out_ref, proj, w_rows, keys_t = refs[chunks:]
    c = pl.program_id(0)
    me = me_ref[0]
    nodes = chunk * chunks

    @pl.when(c == 0)
    def _():
        for b in range(pieces):
            w_rows[b * piece_rows:(b + 1) * piece_rows, :] = w_ref[(b - me_ref[1] + pieces) % pieces]
        for j in range(chunks):
            proj[j * chunk:(j + 1) * chunk, :] = jnp.dot(
                chunk_refs[j][...], w_rows[...], preferred_element_type=jnp.float32
            ).astype(proj.dtype)
        for h in range(heads):
            base = h * 3 * HEAD_DIM
            keys_t[h] = proj[:, base + HEAD_DIM:base + 2 * HEAD_DIM].T

    start = pl.multiple_of(((c - me + chunks) % chunks) * chunk, TILE)
    per_chunk = chunk // TILE
    first = (c * chunk) // BLOCK
    split_row = (first + 1) * BLOCK - c * chunk
    lane_tile = lax.broadcasted_iota(jnp.int32, (1, nodes), 1) // TILE
    lanes_a = jnp.zeros((1, nodes), jnp.int32)
    lanes_b = jnp.zeros((1, nodes), jnp.int32)
    second = jnp.minimum(first + 1, blocks - 1)
    for t in range(nodes // TILE):
        node = ((me + t // per_chunk) % chunks) * chunk + (t % per_chunk) * TILE
        lanes_a = jnp.where(lane_tile == t, mask_ref[first * blocks + node // BLOCK], lanes_a)
        lanes_b = jnp.where(lane_tile == t, mask_ref[second * blocks + node // BLOCK], lanes_b)
    row = lax.broadcasted_iota(jnp.int32, (chunk, 1), 0)
    allowed = jnp.where(row < split_row, lanes_a, lanes_b) > 0
    rows = proj[pl.ds(start, chunk), :]
    scale = 1.0 / math.sqrt(HEAD_DIM)
    for h in range(heads):
        base = h * 3 * HEAD_DIM
        q = rows[:, base:base + HEAD_DIM]
        v = proj[:, base + 2 * HEAD_DIM:base + 3 * HEAD_DIM]
        scores = jnp.dot(q, keys_t[h], preferred_element_type=jnp.float32) * scale
        scores = jnp.where(allowed, scores, -1e30)
        top = jnp.max(scores, axis=-1, keepdims=True)
        weights = jnp.exp(scores - top)
        inverse = 1.0 / jnp.sum(weights, axis=-1, keepdims=True)
        probs = (weights * inverse).astype(jnp.bfloat16)
        out = jnp.dot(probs, v, preferred_element_type=jnp.float32)
        out_ref[:, h * HEAD_DIM:(h + 1) * HEAD_DIM] = out.astype(out_ref.dtype)


def attention(me, mask, chunk_list, w_stack):
    chunks = len(chunk_list)
    chunk, width = chunk_list[0].shape
    pieces, piece_rows, cols = w_stack.shape
    nodes = chunk * chunks
    heads = cols // (3 * HEAD_DIM)
    blocks = mask.shape[-1]
    kernel = functools.partial(
        attention_kernel, chunk=chunk, chunks=chunks, heads=heads, blocks=blocks, width=width,
        pieces=pieces, piece_rows=piece_rows,
    )
    whole = lambda c, me, mask: (0, 0)
    return pl.pallas_call(
        kernel,
        out_shape=jax.ShapeDtypeStruct((nodes, heads * HEAD_DIM), jnp.bfloat16),
        grid_spec=pltpu.PrefetchScalarGridSpec(
            num_scalar_prefetch=2,
            grid=(chunks,),
            in_specs=[pl.BlockSpec((chunk, width), whole)] * chunks
            + [pl.BlockSpec((pieces, piece_rows, cols), lambda c, me, mask: (0, 0, 0))],
            out_specs=pl.BlockSpec((chunk, heads * HEAD_DIM), lambda c, me, mask: (c, 0)),
            scratch_shapes=[
                pltpu.VMEM((nodes, cols), jnp.bfloat16),
                pltpu.VMEM((pieces * piece_rows, cols), jnp.bfloat16),
                pltpu.VMEM((heads, HEAD_DIM, nodes), jnp.bfloat16),
            ],
        ),
    )(me, mask.reshape(-1), *chunk_list, w_stack)


def ring_gather(pieces, axes, counts):
    relatives = [[piece] + [None] * (count - 1) for piece, count in zip(pieces, counts)]
    moving = [[piece, piece] for piece in pieces]
    for step in range(1, max(counts) // 2 + 1):
        for which, (axis, count) in enumerate(zip(axes, counts)):
            if step > count // 2:
                continue
            right = [(i, (i + 1) % count) for i in range(count)]
            left = [(i, (i - 1) % count) for i in range(count)]
            moving[which][0] = lax.ppermute(moving[which][0], axis, right)
            relatives[which][(count - step) % count] = moving[which][0]
            if step < count - step:
                moving[which][1] = lax.ppermute(moving[which][1], axis, left)
                relatives[which][step] = moving[which][1]
        moving = lax.optimization_barrier(moving)
        for which, count in enumerate(counts):
            if step <= count // 2:
                relatives[which][(count - step) % count] = moving[which][0]
                if step < count - step:
                    relatives[which][step] = moving[which][1]
    return relatives


def per_device(
    node_features, block_mask, w_qkv, w_out, norm_gain, routes, gates, w_gate_up, w_down
):
    feats = node_features[0]
    node_dev, width = feats.shape
    seq_count = lax.axis_size("seq")
    exp_count = lax.axis_size("exp")
    experts = seq_count * exp_count * w_gate_up.shape[0]
    head_cols = w_qkv.shape[1]
    out_all = lax.all_gather(w_out[None], ("seq", "exp"), axis=0, tiled=True)
    col_pieces, chunks = ring_gather((w_qkv, feats), ("exp", "seq"), (exp_count, seq_count))
    me = jnp.stack([lax.axis_index("seq"), lax.axis_index("exp")]).astype(jnp.int32)
    attended = attention(me, block_mask[0], chunks, jnp.stack(col_pieces))
    node_attended = lax.all_to_all(attended, "seq", split_axis=0, concat_axis=1, tiled=True)
    out_tiles = out_all.reshape(seq_count, exp_count, w_out.shape[0], w_out.shape[1])
    attn_out = jnp.einsum(
        "nsk,sekc->nec",
        node_attended.reshape(node_dev, seq_count, w_out.shape[0]),
        out_tiles,
        preferred_element_type=jnp.float32,
    )
    mixed = feats.astype(jnp.float32) + attn_out.reshape(node_dev, width)
    mean_square = jnp.mean(mixed * mixed, axis=-1, keepdims=True)
    normed = (mixed * lax.rsqrt(mean_square + 1e-06) * norm_gain).astype(jnp.bfloat16)
    capacity = 2 * TOP * node_dev // experts
    pair_routes = routes[0].reshape(node_dev * TOP)
    onehot = (pair_routes[:, None] == jnp.arange(experts, dtype=jnp.int32)).astype(jnp.int32)
    earlier = jnp.cumsum(onehot, axis=0, dtype=jnp.int32) - onehot
    slots = jnp.sum(earlier * onehot, axis=1, dtype=jnp.int32)
    position = (pair_routes * capacity + slots).reshape(node_dev, TOP)
    places = jnp.arange(experts * capacity, dtype=jnp.int32)
    select = (places[:, None, None] == position[None]).astype(jnp.bfloat16)
    outgoing = jnp.dot(
        jnp.sum(select, axis=2), normed, preferred_element_type=jnp.float32
    ).astype(jnp.bfloat16)
    hidden_units = w_down.shape[1]
    lanes = 128
    packed = (experts, capacity * width // lanes, lanes)
    received = lax.all_to_all(
        outgoing.reshape(packed), ("seq", "exp"), split_axis=0, concat_axis=0, tiled=True
    ).reshape(experts * capacity, width)
    both = jnp.dot(received, w_gate_up[0], preferred_element_type=jnp.float32)
    hidden = (jax.nn.silu(both[:, :hidden_units]) * both[:, hidden_units:]).astype(jnp.bfloat16)
    processed = jnp.dot(hidden, w_down[0], preferred_element_type=jnp.float32).astype(jnp.bfloat16)
    returned = lax.all_to_all(
        processed.reshape(packed), ("seq", "exp"), split_axis=0, concat_axis=0, tiled=True
    ).reshape(experts * capacity, width)
    picked = jnp.einsum("pnk,pd->knd", select, returned, preferred_element_type=jnp.float32)
    expert_sum = picked[0] * gates[0][:, 0, None] + picked[1] * gates[0][:, 1, None]
    return (mixed + expert_sum).astype(jnp.bfloat16)[None]


def solution(mesh):
    in_specs = (
        P(("sub", "exp"), "seq", None),
        P(("sub", "exp"), None, None),
        P("exp", "seq"),
        P("seq", "exp"),
        P(),
        P(("sub", "exp"), "seq", None),
        P(("sub", "exp"), "seq", None),
        P(("seq", "exp"), None, None),
        P(("seq", "exp"), None, None),
    )
    out_specs = P(("sub", "exp"), "seq", None)
    return jax.shard_map(
        per_device, mesh=mesh, in_specs=in_specs, out_specs=out_specs, check_vma=False
    )
```

```python
import functools
import math

import jax
import jax.numpy as jnp
from jax import lax
from jax.experimental import pallas as pl
from jax.experimental.pallas import tpu as pltpu
from jax.sharding import PartitionSpec as P

HEAD_DIM = 64
TOP = 2
BLOCK = 128
TILE = 64


def attention_kernel(
    me_ref, mask_ref, *refs, chunk, chunks, heads, blocks, width, pieces, piece_rows
):
    chunk_refs = refs[:chunks]
    w_ref, out_ref, proj, w_rows, keys_t = refs[chunks:]
    c = pl.program_id(0)
    me = me_ref[0]
    nodes = chunk * chunks

    @pl.when(c == 0)
    def _():
        for b in range(pieces):
            w_rows[b * piece_rows:(b + 1) * piece_rows, :] = w_ref[(b - me_ref[1] + pieces) % pieces]
        for j in range(chunks):
            proj[j * chunk:(j + 1) * chunk, :] = jnp.dot(
                chunk_refs[j][...], w_rows[...], preferred_element_type=jnp.float32
            ).astype(proj.dtype)
        for h in range(heads):
            base = h * 3 * HEAD_DIM
            keys_t[h] = proj[:, base + HEAD_DIM:base + 2 * HEAD_DIM].T

    start = pl.multiple_of(((c - me + chunks) % chunks) * chunk, TILE)
    per_chunk = chunk // TILE
    first = (c * chunk) // BLOCK
    split_row = (first + 1) * BLOCK - c * chunk
    lane_tile = lax.broadcasted_iota(jnp.int32, (1, nodes), 1) // TILE
    lanes_a = jnp.zeros((1, nodes), jnp.int32)
    lanes_b = jnp.zeros((1, nodes), jnp.int32)
    second = jnp.minimum(first + 1, blocks - 1)
    for t in range(nodes // TILE):
        node = ((me + t // per_chunk) % chunks) * chunk + (t % per_chunk) * TILE
        lanes_a = jnp.where(lane_tile == t, mask_ref[first * blocks + node // BLOCK], lanes_a)
        lanes_b = jnp.where(lane_tile == t, mask_ref[second * blocks + node // BLOCK], lanes_b)
    row = lax.broadcasted_iota(jnp.int32, (chunk, 1), 0)
    allowed = jnp.where(row < split_row, lanes_a, lanes_b) > 0
    rows = proj[pl.ds(start, chunk), :]
    scale = 1.0 / math.sqrt(HEAD_DIM)
    for h in range(heads):
        base = h * 3 * HEAD_DIM
        q = rows[:, base:base + HEAD_DIM]
        v = proj[:, base + 2 * HEAD_DIM:base + 3 * HEAD_DIM]
        scores = jnp.dot(q, keys_t[h], preferred_element_type=jnp.float32) * scale
        scores = jnp.where(allowed, scores, -1e30)
        top = jnp.max(scores, axis=-1, keepdims=True)
        weights = jnp.exp(scores - top)
        inverse = 1.0 / jnp.sum(weights, axis=-1, keepdims=True)
        probs = (weights * inverse).astype(jnp.bfloat16)
        out = jnp.dot(probs, v, preferred_element_type=jnp.float32)
        out_ref[:, h * HEAD_DIM:(h + 1) * HEAD_DIM] = out.astype(out_ref.dtype)


def attention(me, mask, chunk_list, w_stack):
    chunks = len(chunk_list)
    chunk, width = chunk_list[0].shape
    pieces, piece_rows, cols = w_stack.shape
    nodes = chunk * chunks
    heads = cols // (3 * HEAD_DIM)
    blocks = mask.shape[-1]
    kernel = functools.partial(
        attention_kernel, chunk=chunk, chunks=chunks, heads=heads, blocks=blocks, width=width,
        pieces=pieces, piece_rows=piece_rows,
    )
    whole = lambda c, me, mask: (0, 0)
    return pl.pallas_call(
        kernel,
        out_shape=jax.ShapeDtypeStruct((nodes, heads * HEAD_DIM), jnp.bfloat16),
        grid_spec=pltpu.PrefetchScalarGridSpec(
            num_scalar_prefetch=2,
            grid=(chunks,),
            in_specs=[pl.BlockSpec((chunk, width), whole)] * chunks
            + [pl.BlockSpec((pieces, piece_rows, cols), lambda c, me, mask: (0, 0, 0))],
            out_specs=pl.BlockSpec((chunk, heads * HEAD_DIM), lambda c, me, mask: (c, 0)),
            scratch_shapes=[
                pltpu.VMEM((nodes, cols), jnp.bfloat16),
                pltpu.VMEM((pieces * piece_rows, cols), jnp.bfloat16),
                pltpu.VMEM((heads, HEAD_DIM, nodes), jnp.bfloat16),
            ],
        ),
    )(me, mask.reshape(-1), *chunk_list, w_stack)


def ring_gather(pieces, axes, counts):
    relatives = [[piece] + [None] * (count - 1) for piece, count in zip(pieces, counts)]
    moving = [[piece, piece] for piece in pieces]
    for step in range(1, max(counts) // 2 + 1):
        for which, (axis, count) in enumerate(zip(axes, counts)):
            if step > count // 2:
                continue
            right = [(i, (i + 1) % count) for i in range(count)]
            left = [(i, (i - 1) % count) for i in range(count)]
            moving[which][0] = lax.ppermute(moving[which][0], axis, right)
            relatives[which][(count - step) % count] = moving[which][0]
            if step < count - step:
                moving[which][1] = lax.ppermute(moving[which][1], axis, left)
                relatives[which][step] = moving[which][1]
        moving = lax.optimization_barrier(moving)
        for which, count in enumerate(counts):
            if step <= count // 2:
                relatives[which][(count - step) % count] = moving[which][0]
                if step < count - step:
                    relatives[which][step] = moving[which][1]
    return relatives


def per_device(
    node_features, block_mask, w_qkv, w_out, norm_gain, routes, gates, w_gate_up, w_down
):
    feats = node_features[0]
    node_dev, width = feats.shape
    seq_count = lax.axis_size("seq")
    exp_count = lax.axis_size("exp")
    experts = seq_count * exp_count * w_gate_up.shape[0]
    head_cols = w_qkv.shape[1]
    out_all = lax.all_gather(w_out[None], ("seq", "exp"), axis=0, tiled=True)
    col_pieces, chunks = ring_gather((w_qkv, feats), ("exp", "seq"), (exp_count, seq_count))
    me = jnp.stack([lax.axis_index("seq"), lax.axis_index("exp")]).astype(jnp.int32)
    attended = attention(me, block_mask[0], chunks, jnp.stack(col_pieces))
    node_attended = lax.all_to_all(attended, "seq", split_axis=0, concat_axis=1, tiled=True)
    out_tiles = out_all.reshape(seq_count, exp_count, w_out.shape[0], w_out.shape[1])
    attn_out = jnp.einsum(
        "nsk,sekc->nec",
        node_attended.reshape(node_dev, seq_count, w_out.shape[0]),
        out_tiles,
        preferred_element_type=jnp.float32,
    )
    mixed = feats.astype(jnp.float32) + attn_out.reshape(node_dev, width)
    mean_square = jnp.mean(mixed * mixed, axis=-1, keepdims=True)
    normed = (mixed * lax.rsqrt(mean_square + 1e-06) * norm_gain).astype(jnp.bfloat16)
    capacity = 2 * TOP * node_dev // experts
    pair_routes = routes[0].reshape(node_dev * TOP)
    onehot = (pair_routes[:, None] == jnp.arange(experts, dtype=jnp.int32)).astype(jnp.int32)
    earlier = jnp.cumsum(onehot, axis=0, dtype=jnp.int32) - onehot
    slots = jnp.sum(earlier * onehot, axis=1, dtype=jnp.int32)
    position = (pair_routes * capacity + slots).reshape(node_dev, TOP)
    places = jnp.arange(experts * capacity, dtype=jnp.int32)
    select = (places[:, None, None] == position[None]).astype(jnp.bfloat16)
    lanes = 128
    packed = (experts, capacity * width // lanes, lanes)
    outgoing = jnp.einsum(
        "pn,njl->pjl",
        jnp.sum(select, axis=2),
        normed.reshape(node_dev, width // lanes, lanes),
        preferred_element_type=jnp.float32,
    ).reshape(packed).astype(jnp.bfloat16)
    hidden_units = w_down.shape[1]
    received = lax.all_to_all(
        outgoing, ("seq", "exp"), split_axis=0, concat_axis=0, tiled=True
    ).reshape(experts * capacity, width)
    both = jnp.dot(received, w_gate_up[0], preferred_element_type=jnp.float32)
    hidden = (jax.nn.silu(both[:, :hidden_units]) * both[:, hidden_units:]).astype(jnp.bfloat16)
    processed = jnp.dot(hidden, w_down[0], preferred_element_type=jnp.float32).astype(jnp.bfloat16)
    returned = lax.all_to_all(
        processed.reshape(packed), ("seq", "exp"), split_axis=0, concat_axis=0, tiled=True
    ).reshape(experts * capacity, width)
    picked = jnp.einsum("pnk,pd->knd", select, returned, preferred_element_type=jnp.float32)
    expert_sum = picked[0] * gates[0][:, 0, None] + picked[1] * gates[0][:, 1, None]
    return (mixed + expert_sum).astype(jnp.bfloat16)[None]


def solution(mesh):
    in_specs = (
        P(("sub", "exp"), "seq", None),
        P(("sub", "exp"), None, None),
        P("exp", "seq"),
        P("seq", "exp"),
        P(),
        P(("sub", "exp"), "seq", None),
        P(("sub", "exp"), "seq", None),
        P(("seq", "exp"), None, None),
        P(("seq", "exp"), None, None),
    )
    out_specs = P(("sub", "exp"), "seq", None)
    return jax.shard_map(
        per_device, mesh=mesh, in_specs=in_specs, out_specs=out_specs, check_vma=False
    )
```

```python
import functools
import math

import jax
import jax.numpy as jnp
from jax import lax
from jax.experimental import pallas as pl
from jax.experimental.pallas import tpu as pltpu
from jax.sharding import PartitionSpec as P

HEAD_DIM = 64
TOP = 2
BLOCK = 128
TILE = 64


def attention_kernel(
    me_ref, mask_ref, *refs, chunk, chunks, heads, blocks, width, pieces, piece_rows
):
    chunk_refs = refs[:chunks]
    w_ref, out_ref, proj, w_rows, keys_t = refs[chunks:]
    c = pl.program_id(0)
    me = me_ref[0]
    nodes = chunk * chunks

    @pl.when(c == 0)
    def _():
        for b in range(pieces):
            w_rows[b * piece_rows:(b + 1) * piece_rows, :] = w_ref[(b - me_ref[1] + pieces) % pieces]
        for j in range(chunks):
            proj[j * chunk:(j + 1) * chunk, :] = jnp.dot(
                chunk_refs[j][...], w_rows[...], preferred_element_type=jnp.float32
            ).astype(proj.dtype)
        for h in range(heads):
            base = h * 3 * HEAD_DIM
            keys_t[h] = proj[:, base + HEAD_DIM:base + 2 * HEAD_DIM].T

    start = pl.multiple_of(((c - me + chunks) % chunks) * chunk, TILE)
    per_chunk = chunk // TILE
    first = (c * chunk) // BLOCK
    split_row = (first + 1) * BLOCK - c * chunk
    lane_tile = lax.broadcasted_iota(jnp.int32, (1, nodes), 1) // TILE
    lanes_a = jnp.zeros((1, nodes), jnp.int32)
    lanes_b = jnp.zeros((1, nodes), jnp.int32)
    second = jnp.minimum(first + 1, blocks - 1)
    for t in range(nodes // TILE):
        node = ((me + t // per_chunk) % chunks) * chunk + (t % per_chunk) * TILE
        lanes_a = jnp.where(lane_tile == t, mask_ref[first * blocks + node // BLOCK], lanes_a)
        lanes_b = jnp.where(lane_tile == t, mask_ref[second * blocks + node // BLOCK], lanes_b)
    row = lax.broadcasted_iota(jnp.int32, (chunk, 1), 0)
    allowed = jnp.where(row < split_row, lanes_a, lanes_b) > 0
    rows = proj[pl.ds(start, chunk), :]
    scale = 1.0 / math.sqrt(HEAD_DIM)
    for h in range(heads):
        base = h * 3 * HEAD_DIM
        q = rows[:, base:base + HEAD_DIM]
        v = proj[:, base + 2 * HEAD_DIM:base + 3 * HEAD_DIM]
        scores = jnp.dot(q, keys_t[h], preferred_element_type=jnp.float32) * scale
        scores = jnp.where(allowed, scores, -1e30)
        top = jnp.max(scores, axis=-1, keepdims=True)
        weights = jnp.exp(scores - top)
        inverse = 1.0 / jnp.sum(weights, axis=-1, keepdims=True)
        probs = (weights * inverse).astype(jnp.bfloat16)
        out = jnp.dot(probs, v, preferred_element_type=jnp.float32)
        out_ref[:, h * HEAD_DIM:(h + 1) * HEAD_DIM] = out.astype(out_ref.dtype)


def attention(me, mask, chunk_list, w_stack):
    chunks = len(chunk_list)
    chunk, width = chunk_list[0].shape
    pieces, piece_rows, cols = w_stack.shape
    nodes = chunk * chunks
    heads = cols // (3 * HEAD_DIM)
    blocks = mask.shape[-1]
    kernel = functools.partial(
        attention_kernel, chunk=chunk, chunks=chunks, heads=heads, blocks=blocks, width=width,
        pieces=pieces, piece_rows=piece_rows,
    )
    whole = lambda c, me, mask: (0, 0)
    return pl.pallas_call(
        kernel,
        out_shape=jax.ShapeDtypeStruct((nodes, heads * HEAD_DIM), jnp.bfloat16),
        grid_spec=pltpu.PrefetchScalarGridSpec(
            num_scalar_prefetch=2,
            grid=(chunks,),
            in_specs=[pl.BlockSpec((chunk, width), whole)] * chunks
            + [pl.BlockSpec((pieces, piece_rows, cols), lambda c, me, mask: (0, 0, 0))],
            out_specs=pl.BlockSpec((chunk, heads * HEAD_DIM), lambda c, me, mask: (c, 0)),
            scratch_shapes=[
                pltpu.VMEM((nodes, cols), jnp.bfloat16),
                pltpu.VMEM((pieces * piece_rows, cols), jnp.bfloat16),
                pltpu.VMEM((heads, HEAD_DIM, nodes), jnp.bfloat16),
            ],
        ),
    )(me, mask.reshape(-1), *chunk_list, w_stack)


def ring_gather(pieces, axes, counts):
    relatives = [[piece] + [None] * (count - 1) for piece, count in zip(pieces, counts)]
    moving = [[piece, piece] for piece in pieces]
    for step in range(1, max(counts) // 2 + 1):
        for which, (axis, count) in enumerate(zip(axes, counts)):
            if step > count // 2:
                continue
            right = [(i, (i + 1) % count) for i in range(count)]
            left = [(i, (i - 1) % count) for i in range(count)]
            moving[which][0] = lax.ppermute(moving[which][0], axis, right)
            relatives[which][(count - step) % count] = moving[which][0]
            if step < count - step:
                moving[which][1] = lax.ppermute(moving[which][1], axis, left)
                relatives[which][step] = moving[which][1]
        moving = lax.optimization_barrier(moving)
        for which, count in enumerate(counts):
            if step <= count // 2:
                relatives[which][(count - step) % count] = moving[which][0]
                if step < count - step:
                    relatives[which][step] = moving[which][1]
    return relatives


def per_device(
    node_features, block_mask, w_qkv, w_out, norm_gain, routes, gates, w_gate_up, w_down
):
    feats = node_features[0]
    node_dev, width = feats.shape
    seq_count = lax.axis_size("seq")
    exp_count = lax.axis_size("exp")
    experts = seq_count * exp_count * w_gate_up.shape[0]
    head_cols = w_qkv.shape[1]
    out_all = lax.all_gather(w_out[None], ("seq", "exp"), axis=0, tiled=True)
    col_pieces, chunks = ring_gather((w_qkv, feats), ("exp", "seq"), (exp_count, seq_count))
    me = jnp.stack([lax.axis_index("seq"), lax.axis_index("exp")]).astype(jnp.int32)
    attended = attention(me, block_mask[0], chunks, jnp.stack(col_pieces))
    node_attended = lax.all_to_all(attended, "seq", split_axis=0, concat_axis=1, tiled=True)
    out_tiles = out_all.reshape(seq_count, exp_count, w_out.shape[0], w_out.shape[1])
    attn_out = jnp.einsum(
        "nsk,sekc->nec",
        node_attended.reshape(node_dev, seq_count, w_out.shape[0]),
        out_tiles,
        preferred_element_type=jnp.float32,
    )
    mixed = feats.astype(jnp.float32) + attn_out.reshape(node_dev, width)
    mean_square = jnp.mean(mixed * mixed, axis=-1, keepdims=True)
    normed = (mixed * lax.rsqrt(mean_square + 1e-06) * norm_gain).astype(jnp.bfloat16)
    capacity = 2 * TOP * node_dev // experts
    pair_routes = routes[0].reshape(node_dev * TOP)
    onehot = (pair_routes[:, None] == jnp.arange(experts, dtype=jnp.int32)).astype(jnp.int32)
    earlier = jnp.cumsum(onehot, axis=0, dtype=jnp.int32) - onehot
    slots = jnp.sum(earlier * onehot, axis=1, dtype=jnp.int32)
    position = (pair_routes * capacity + slots).reshape(node_dev, TOP)
    places = jnp.arange(experts * capacity, dtype=jnp.int32)
    select = (places[:, None, None] == position[None]).astype(jnp.bfloat16)
    lanes = 128
    packed = (experts, capacity * width // lanes, lanes)
    outgoing = jnp.einsum(
        "pn,njl->pjl",
        jnp.sum(select, axis=2),
        normed.reshape(node_dev, width // lanes, lanes),
        preferred_element_type=jnp.float32,
    ).reshape(packed).astype(jnp.bfloat16)
    hidden_units = w_down.shape[1]
    received = lax.all_to_all(
        outgoing, ("seq", "exp"), split_axis=0, concat_axis=0, tiled=True
    ).reshape(experts * capacity, width // lanes, lanes)
    both = jnp.einsum(
        "pjl,jlf->pf",
        received,
        w_gate_up[0].reshape(width // lanes, lanes, -1),
        preferred_element_type=jnp.float32,
    )
    hidden = (jax.nn.silu(both[:, :hidden_units]) * both[:, hidden_units:]).astype(jnp.bfloat16)
    processed = jnp.einsum(
        "pf,fjl->pjl",
        hidden,
        w_down[0].reshape(hidden_units, width // lanes, lanes),
        preferred_element_type=jnp.float32,
    ).astype(jnp.bfloat16)
    returned = lax.all_to_all(
        processed.reshape(packed), ("seq", "exp"), split_axis=0, concat_axis=0, tiled=True
    ).reshape(experts * capacity, width // lanes, lanes)
    picked = jnp.einsum(
        "pnk,pjl->knjl", select, returned, preferred_element_type=jnp.float32
    ).reshape(TOP, node_dev, width)
    expert_sum = picked[0] * gates[0][:, 0, None] + picked[1] * gates[0][:, 1, None]
    return (mixed + expert_sum).astype(jnp.bfloat16)[None]


def solution(mesh):
    in_specs = (
        P(("sub", "exp"), "seq", None),
        P(("sub", "exp"), None, None),
        P("exp", "seq"),
        P("seq", "exp"),
        P(),
        P(("sub", "exp"), "seq", None),
        P(("sub", "exp"), "seq", None),
        P(("seq", "exp"), None, None),
        P(("seq", "exp"), None, None),
    )
    out_specs = P(("sub", "exp"), "seq", None)
    return jax.shard_map(
        per_device, mesh=mesh, in_specs=in_specs, out_specs=out_specs, check_vma=False
    )
```

```python
import functools
import math

import jax
import jax.numpy as jnp
from jax import lax
from jax.experimental import pallas as pl
from jax.experimental.pallas import tpu as pltpu
from jax.sharding import PartitionSpec as P

HEAD_DIM = 64
TOP = 2
BLOCK = 128
TILE = 64


def attention_kernel(
    me_ref, mask_ref, *refs, chunk, chunks, heads, blocks, width, pieces, piece_rows
):
    chunk_refs = refs[:chunks]
    w_ref, out_ref, proj, w_rows, keys_t = refs[chunks:]
    c = pl.program_id(0)
    me = me_ref[0]
    nodes = chunk * chunks

    @pl.when(c == 0)
    def _():
        for b in range(pieces):
            w_rows[b * piece_rows:(b + 1) * piece_rows, :] = w_ref[(b - me_ref[1] + pieces) % pieces]
        for j in range(chunks):
            proj[j * chunk:(j + 1) * chunk, :] = jnp.dot(
                chunk_refs[j][...], w_rows[...], preferred_element_type=jnp.float32
            ).astype(proj.dtype)
        for h in range(heads):
            base = h * 3 * HEAD_DIM
            keys_t[h] = proj[:, base + HEAD_DIM:base + 2 * HEAD_DIM].T

    start = pl.multiple_of(((c - me + chunks) % chunks) * chunk, TILE)
    per_chunk = chunk // TILE
    first = (c * chunk) // BLOCK
    split_row = (first + 1) * BLOCK - c * chunk
    lane_tile = lax.broadcasted_iota(jnp.int32, (1, nodes), 1) // TILE
    lanes_a = jnp.zeros((1, nodes), jnp.int32)
    lanes_b = jnp.zeros((1, nodes), jnp.int32)
    second = jnp.minimum(first + 1, blocks - 1)
    for t in range(nodes // TILE):
        node = ((me + t // per_chunk) % chunks) * chunk + (t % per_chunk) * TILE
        lanes_a = jnp.where(lane_tile == t, mask_ref[first * blocks + node // BLOCK], lanes_a)
        lanes_b = jnp.where(lane_tile == t, mask_ref[second * blocks + node // BLOCK], lanes_b)
    row = lax.broadcasted_iota(jnp.int32, (chunk, 1), 0)
    allowed = jnp.where(row < split_row, lanes_a, lanes_b) > 0
    rows = proj[pl.ds(start, chunk), :]
    scale = 1.0 / math.sqrt(HEAD_DIM)
    for h in range(heads):
        base = h * 3 * HEAD_DIM
        q = rows[:, base:base + HEAD_DIM]
        v = proj[:, base + 2 * HEAD_DIM:base + 3 * HEAD_DIM]
        scores = jnp.dot(q, keys_t[h], preferred_element_type=jnp.float32) * scale
        scores = jnp.where(allowed, scores, -1e30)
        top = jnp.max(scores, axis=-1, keepdims=True)
        weights = jnp.exp(scores - top)
        inverse = 1.0 / jnp.sum(weights, axis=-1, keepdims=True)
        probs = (weights * inverse).astype(jnp.bfloat16)
        out = jnp.dot(probs, v, preferred_element_type=jnp.float32)
        out_ref[:, h * HEAD_DIM:(h + 1) * HEAD_DIM] = out.astype(out_ref.dtype)


def attention(me, mask, chunk_list, w_stack):
    chunks = len(chunk_list)
    chunk, width = chunk_list[0].shape
    pieces, piece_rows, cols = w_stack.shape
    nodes = chunk * chunks
    heads = cols // (3 * HEAD_DIM)
    blocks = mask.shape[-1]
    kernel = functools.partial(
        attention_kernel, chunk=chunk, chunks=chunks, heads=heads, blocks=blocks, width=width,
        pieces=pieces, piece_rows=piece_rows,
    )
    whole = lambda c, me, mask: (0, 0)
    return pl.pallas_call(
        kernel,
        out_shape=jax.ShapeDtypeStruct((nodes, heads * HEAD_DIM), jnp.bfloat16),
        grid_spec=pltpu.PrefetchScalarGridSpec(
            num_scalar_prefetch=2,
            grid=(chunks,),
            in_specs=[pl.BlockSpec((chunk, width), whole)] * chunks
            + [pl.BlockSpec((pieces, piece_rows, cols), lambda c, me, mask: (0, 0, 0))],
            out_specs=pl.BlockSpec((chunk, heads * HEAD_DIM), lambda c, me, mask: (c, 0)),
            scratch_shapes=[
                pltpu.VMEM((nodes, cols), jnp.bfloat16),
                pltpu.VMEM((pieces * piece_rows, cols), jnp.bfloat16),
                pltpu.VMEM((heads, HEAD_DIM, nodes), jnp.bfloat16),
            ],
        ),
    )(me, mask.reshape(-1), *chunk_list, w_stack)


def ring_gather(pieces, axes, counts):
    relatives = [[piece] + [None] * (count - 1) for piece, count in zip(pieces, counts)]
    moving = [[piece, piece] for piece in pieces]
    for step in range(1, max(counts) // 2 + 1):
        for which, (axis, count) in enumerate(zip(axes, counts)):
            if step > count // 2:
                continue
            right = [(i, (i + 1) % count) for i in range(count)]
            left = [(i, (i - 1) % count) for i in range(count)]
            moving[which][0] = lax.ppermute(moving[which][0], axis, right)
            relatives[which][(count - step) % count] = moving[which][0]
            if step < count - step:
                moving[which][1] = lax.ppermute(moving[which][1], axis, left)
                relatives[which][step] = moving[which][1]
        moving = lax.optimization_barrier(moving)
        for which, count in enumerate(counts):
            if step <= count // 2:
                relatives[which][(count - step) % count] = moving[which][0]
                if step < count - step:
                    relatives[which][step] = moving[which][1]
    return relatives


def per_device(
    node_features, block_mask, w_qkv, w_out, norm_gain, routes, gates, w_gate_up, w_down
):
    feats = node_features[0]
    node_dev, width = feats.shape
    seq_count = lax.axis_size("seq")
    exp_count = lax.axis_size("exp")
    experts = seq_count * exp_count * w_gate_up.shape[0]
    head_cols = w_qkv.shape[1]
    out_all = lax.all_gather(w_out[None], ("seq", "exp"), axis=0, tiled=True)
    col_pieces, chunks = ring_gather((w_qkv, feats), ("exp", "seq"), (exp_count, seq_count))
    me = jnp.stack([lax.axis_index("seq"), lax.axis_index("exp")]).astype(jnp.int32)
    attended = attention(me, block_mask[0], chunks, jnp.stack(col_pieces))
    node_attended = lax.all_to_all(attended, "seq", split_axis=0, concat_axis=1, tiled=True)
    out_tiles = out_all.reshape(seq_count, exp_count, w_out.shape[0], w_out.shape[1])
    attn_out = jnp.einsum(
        "nsk,sekc->nec",
        node_attended.reshape(node_dev, seq_count, w_out.shape[0]),
        out_tiles,
        preferred_element_type=jnp.float32,
    )
    mixed = feats.astype(jnp.float32) + attn_out.reshape(node_dev, width)
    mean_square = jnp.mean(mixed * mixed, axis=-1, keepdims=True)
    normed = (mixed * lax.rsqrt(mean_square + 1e-06) * norm_gain).astype(jnp.bfloat16)
    capacity = 2 * TOP * node_dev // experts
    pair_routes = routes[0].reshape(node_dev * TOP)
    onehot = (pair_routes[:, None] == jnp.arange(experts, dtype=jnp.int32)).astype(jnp.int32)
    earlier = jnp.cumsum(onehot, axis=0, dtype=jnp.int32) - onehot
    slots = jnp.sum(earlier * onehot, axis=1, dtype=jnp.int32)
    position = (pair_routes * capacity + slots).reshape(node_dev, TOP)
    places = jnp.arange(experts * capacity, dtype=jnp.int32)
    select = (places[:, None, None] == position[None]).astype(jnp.bfloat16)
    lanes = 128
    packed = (experts, capacity * width // lanes, lanes)
    outgoing = jnp.einsum(
        "pn,njl->pjl",
        jnp.sum(select, axis=2),
        normed.reshape(node_dev, width // lanes, lanes),
        preferred_element_type=jnp.float32,
    ).reshape(packed).astype(jnp.bfloat16)
    hidden_units = w_down.shape[1]
    received = lax.all_to_all(
        outgoing, ("seq", "exp"), split_axis=0, concat_axis=0, tiled=True
    ).reshape(experts * capacity, width // lanes, lanes)
    both = jnp.einsum(
        "pjl,jlf->pf",
        received,
        w_gate_up[0].reshape(width // lanes, lanes, -1),
        preferred_element_type=jnp.float32,
    )
    hidden = (jax.nn.silu(both[:, :hidden_units]) * both[:, hidden_units:]).astype(jnp.bfloat16)
    processed = jnp.einsum(
        "pf,fjl->pjl",
        hidden,
        w_down[0].reshape(hidden_units, width // lanes, lanes),
        preferred_element_type=jnp.float32,
    ).astype(jnp.bfloat16)
    returned = lax.all_to_all(
        processed.reshape(packed), ("seq", "exp"), split_axis=0, concat_axis=0, tiled=True
    ).reshape(experts * capacity, width // lanes, lanes)
    picked = [
        jnp.einsum(
            "pn,pjl->njl", select[:, :, k], returned, preferred_element_type=jnp.float32
        ).reshape(node_dev, width)
        for k in range(TOP)
    ]
    expert_sum = picked[0] * gates[0][:, 0, None] + picked[1] * gates[0][:, 1, None]
    return (mixed + expert_sum).astype(jnp.bfloat16)[None]


def solution(mesh):
    in_specs = (
        P(("sub", "exp"), "seq", None),
        P(("sub", "exp"), None, None),
        P("exp", "seq"),
        P("seq", "exp"),
        P(),
        P(("sub", "exp"), "seq", None),
        P(("sub", "exp"), "seq", None),
        P(("seq", "exp"), None, None),
        P(("seq", "exp"), None, None),
    )
    out_specs = P(("sub", "exp"), "seq", None)
    return jax.shard_map(
        per_device, mesh=mesh, in_specs=in_specs, out_specs=out_specs, check_vma=False
    )
```
